512 devices in a mesh: space: 32 (over y_lo, z), field: 16 (over x, y_hi, core).
Axes of the slice: x: 4, y: 8 (y_hi: 2, y_lo: 4; y = y_hi * 4 + y_lo), z: 8, core: 2. Of those that a mesh axis runs over, the one named last changes fastest.
Arguments:
- fields: float32 [16, 1024, 6144], P('field', 'space'), may hold values from -6 to 6
- zone_ids: int32 [1024, 6144], P('space'), may hold values from 0 to 7
- diffusivity: float32 [16, 8], P('field'), may hold values from 0.3 to 3
- heat_rate: float32 [15], replicated, may hold values from 0.3 to 1.5
- weight_in: bfloat16 [384, 16], replicated, may hold values from -1.5 to 1.5
- bias_in: float32 [384], replicated, may hold values from -3 to 3
- weight_mid: bfloat16 [384, 384], replicated, may hold values from -0.3125 to 0.3125
- bias_mid: float32 [384], replicated, may hold values from -3 to 3
- weight_out: bfloat16 [16, 384], replicated, may hold values from -0.3125 to 0.3125
- bias_out: float32 [16], replicated, may hold values from -2 to 2
Outputs:
- new_fields: float32 [16, 1024, 6144], P('field', 'space')
The draws below stay inside these ranges and needn't reach their ends.
All inputs are finite; a program needn't handle non-finite values.
Results may differ from the reference program's by a relative error of at most 0.005.
Values may be sent and summed in bfloat16 or wider, within the bound.
No kernel may reach another device: no remote copies, remote signals or barrier semaphores. Data moves between devices by JAX's collectives and lax.ppermute only.
A program may use at most 64 MiB of HBM per device.

```python
import math
import jax
import jax.numpy as jnp
from jax import lax

FIELDS = 16
COMPS = 15
HID = 384
ZONES = 8
SWEEPS = 3
ROWS_BLK = 1024
NY = 6144
NX = 1024


def set_ends(values, key, smallest, high):
    dims = values.shape
    index_at = [jax.random.randint(jax.random.fold_in(key, axis), (), 0, dims[axis]) for axis in range(len(dims))]
    values = values.at[tuple(index_at)].set(smallest)
    longest = dims.index(max(dims))
    index_at[longest] = (index_at[longest] + 1) % dims[longest]
    return values.at[tuple(index_at)].set(high)


def shard_levels(own_key, extent, shards, smallest, largest):
    level, own = 1.0, jax.random.fold_in(own_key, 6)
    for axis_at, blocks in shards:
        draws = jnp.exp(jax.random.uniform(jax.random.fold_in(own, axis_at), (blocks,), jnp.float32, smallest / len(shards), largest / len(shards)))
        level = level * jnp.repeat(draws, extent[axis_at] // blocks).reshape([-1 if axis == axis_at else 1 for axis in range(len(extent))])
    return level


def noise(own_key, dims, scale, reach, split=(), kind=jnp.bfloat16):
    values = jax.random.normal(own_key, dims, jnp.float32) * scale
    if len(split) > 0:
        values = shard_levels(own_key, dims, split, -0.22, 0.18) * values
    return jnp.clip(values, min=-reach, max=reach).astype(kind)


def setup_inputs(seed: int = 0) -> dict:
    arg_keys = jax.random.split(jax.random.key(seed), 11)
    fields = noise(arg_keys[0], (FIELDS, NX, NY), 1.0, 6.0, ((0, 16), (1, 32)), jnp.float32)
    zone_ids = set_ends(jax.random.randint(arg_keys[1], (NX, NY), 0, ZONES), jax.random.fold_in(arg_keys[1], 1), 0, ZONES - 1).astype(jnp.int32)
    diffusivity = jnp.clip(jnp.exp(math.log(3.0) - 2.3025851 * jax.random.uniform(arg_keys[2], (FIELDS, ZONES), jnp.float32) ** shard_levels(arg_keys[2], (FIELDS, ZONES), ((0, 16),), -0.2, 0.2)), 0.3, 3.0)
    heat_rate = jnp.clip(jnp.exp(jax.random.uniform(arg_keys[3], (COMPS,), jnp.float32, math.log(0.3), math.log(1.5))), 0.3, 1.5)
    weight_in = noise(arg_keys[4], (HID, FIELDS), FIELDS ** -0.5, 1.5)
    bias_in = noise(arg_keys[5], (HID,), 0.5, 3.0, (), jnp.float32)
    weight_mid = noise(arg_keys[6], (HID, HID), HID ** -0.5, 0.3125)
    bias_mid = noise(arg_keys[7], (HID,), 0.5, 3.0, (), jnp.float32)
    weight_out = noise(arg_keys[8], (FIELDS, HID), HID ** -0.5, 0.3125)
    bias_out = noise(arg_keys[9], (FIELDS,), 0.3, 2.0, (), jnp.float32)
    return {"fields": fields, "zone_ids": zone_ids, "diffusivity": diffusivity, "heat_rate": heat_rate, "weight_in": weight_in, "bias_in": bias_in, "weight_mid": weight_mid, "bias_mid": bias_mid, "weight_out": weight_out, "bias_out": bias_out}


RELAX_WEIGHTS = (0.8, 1.25, 0.95)


def relax_step(padded, source, coef_pad, weight):
    middle = padded[:, 1:-1]
    coef_mid = coef_pad[:, 1:-1]
    face_north = 0.5 * (coef_mid + coef_pad[:, 2:])
    face_south = 0.5 * (coef_mid + coef_pad[:, :-2])
    face_east = 0.5 * (coef_mid + jnp.roll(coef_mid, -1, 2))
    face_west = 0.5 * (coef_mid + jnp.roll(coef_mid, 1, 2))
    diagonal = 1.0 + face_north + face_south + face_east + face_west
    image = diagonal * middle - face_north * padded[:, 2:] - face_south * padded[:, :-2]
    image = image - face_east * jnp.roll(middle, -1, 2) - face_west * jnp.roll(middle, 1, 2)
    return middle + weight * (source - image) / diagonal


def lookup(zone_ids, diffusivity):
    coefs = jnp.zeros((diffusivity.shape[0],) + zone_ids.shape, jnp.float32)
    for number in range(diffusivity.shape[1]):
        coefs = coefs + jnp.where((zone_ids == number)[None], diffusivity[:, number][:, None, None], jnp.float32(0.0))
    return coefs


def surrogate(inputs, weight_in, bias_in, weight_mid, bias_mid, weight_out, bias_out):
    hidden = jax.nn.silu(jnp.dot(weight_in, inputs, preferred_element_type=jnp.float32) + bias_in[:, None]).astype(jnp.bfloat16)
    hidden = jax.nn.silu(jnp.dot(weight_mid, hidden, preferred_element_type=jnp.float32) + bias_mid[:, None]).astype(jnp.bfloat16)
    return (jnp.dot(weight_out, hidden, preferred_element_type=jnp.float32) + bias_out[:, None]).astype(jnp.bfloat16)


def pad_rows(array):
    return jnp.pad(array, ((0, 0), (1, 1), (0, 0)))


def reference(fields, zone_ids, diffusivity, heat_rate, weight_in, bias_in, weight_mid, bias_mid, weight_out, bias_out):
    coefs = lookup(zone_ids, diffusivity)
    coef_pad = pad_rows(coefs)
    state = fields
    for number in range(SWEEPS):
        state = relax_step(pad_rows(state), fields, coef_pad, RELAX_WEIGHTS[number])
    cells = NX * NY
    by_block = state.astype(jnp.bfloat16).reshape(FIELDS, cells // ROWS_BLK, ROWS_BLK).transpose(1, 0, 2)

    def apply_block(row_block):
        return surrogate(row_block, weight_in, bias_in, weight_mid, bias_mid, weight_out, bias_out)

    change = lax.map(apply_block, by_block).transpose(1, 0, 2).reshape(FIELDS, NX, NY).astype(jnp.float32)
    new_heat = state[-1] + change[-1]
    factor = jnp.exp(heat_rate[:, None, None] * jnp.tanh(new_heat)[None])
    scaled = (change[:-1] * factor).astype(jnp.bfloat16).astype(jnp.float32)
    species = state[:-1] + scaled
    return jnp.concatenate([species, new_heat[None]], 0)
```

```python
import jax
import jax.numpy as jnp
from jax import lax
from jax.experimental import pallas as pl
from jax.experimental.pallas import tpu as pltpu
from jax.sharding import PartitionSpec as P

FIELDS = 16
SWEEPS = 3
HALO = SWEEPS
CHUNK = 384
ROW_BLOCK = 8

RELAX_WEIGHTS = (0.8, 1.25, 0.95)


def pad_rows(array):
    return jnp.pad(array, ((0, 0), (1, 1), (0, 0)))


def relax_step(padded, source, coef_pad, weight):
    middle = padded[:, 1:-1]
    coef_mid = coef_pad[:, 1:-1]
    face_north = 0.5 * (coef_mid + coef_pad[:, 2:])
    face_south = 0.5 * (coef_mid + coef_pad[:, :-2])
    face_east = 0.5 * (coef_mid + jnp.roll(coef_mid, -1, 2))
    face_west = 0.5 * (coef_mid + jnp.roll(coef_mid, 1, 2))
    diagonal = 1.0 + face_north + face_south + face_east + face_west
    image = diagonal * middle - face_north * padded[:, 2:] - face_south * padded[:, :-2]
    image = image - face_east * jnp.roll(middle, -1, 2) - face_west * jnp.roll(middle, 1, 2)
    return middle + weight * (source - image) / diagonal


def lookup(zone_ids, diffusivity):
    coefs = jnp.zeros((diffusivity.shape[0],) + zone_ids.shape, jnp.float32)
    for number in range(diffusivity.shape[1]):
        coefs = coefs + jnp.where(
            (zone_ids == number)[None], diffusivity[:, number][:, None, None], jnp.float32(0.0)
        )
    return coefs


def with_halo(block, axis, width):
    count = lax.axis_size(axis)
    head = block[:, :width]
    tail = block[:, -width:]
    from_above = lax.ppermute(tail, axis, [(i, i + 1) for i in range(count - 1)])
    from_below = lax.ppermute(head, axis, [(i + 1, i) for i in range(count - 1)])
    return jnp.concatenate([from_above, block, from_below], axis=1)


def surrogate_kernel(x_ref, w_in_ref, b_in_ref, w_mid_ref, b_mid_ref, w_out_ref, b_out_ref, rate_ref, o_ref):
    w_in = w_in_ref[...]
    w_mid = w_mid_ref[...]
    w_out = w_out_ref[...]
    b_in = b_in_ref[...]
    b_mid = b_mid_ref[...]
    b_out = b_out_ref[...]
    rate = rate_ref[...]
    is_heat = lax.broadcasted_iota(jnp.int32, (FIELDS, CHUNK), 0) == FIELDS - 1

    def row(r, carry):
        x = x_ref[r]
        inputs = x.astype(jnp.bfloat16)
        hidden = jax.nn.silu(jnp.dot(w_in, inputs, preferred_element_type=jnp.float32) + b_in)
        hidden = hidden.astype(jnp.bfloat16)
        hidden = jax.nn.silu(jnp.dot(w_mid, hidden, preferred_element_type=jnp.float32) + b_mid)
        hidden = hidden.astype(jnp.bfloat16)
        change = (jnp.dot(w_out, hidden, preferred_element_type=jnp.float32) + b_out).astype(jnp.bfloat16)
        change = change.astype(jnp.float32)
        heat = x[FIELDS - 1 :] + change[FIELDS - 1 :]
        factor = jnp.exp(rate * jnp.tanh(heat))
        scaled = (change * factor).astype(jnp.bfloat16)
        o_ref[r] = jnp.where(is_heat, change.astype(jnp.bfloat16), scaled)
        return carry

    lax.fori_loop(0, x_ref.shape[0], row, 0)


def surrogate(x, weight_in, bias_in, weight_mid, bias_mid, weight_out, bias_out, rate):
    rows = x.shape[0]
    full = lambda shape: pl.BlockSpec(shape, lambda i: (0,) * len(shape))
    return pl.pallas_call(
        surrogate_kernel,
        grid=(rows // ROW_BLOCK,),
        in_specs=[
            pl.BlockSpec((ROW_BLOCK, FIELDS, CHUNK), lambda i: (i, 0, 0)),
            full(weight_in.shape),
            full(bias_in.shape),
            full(weight_mid.shape),
            full(bias_mid.shape),
            full(weight_out.shape),
            full(bias_out.shape),
            full(rate.shape),
        ],
        out_specs=pl.BlockSpec((ROW_BLOCK, FIELDS, CHUNK), lambda i: (i, 0, 0)),
        out_shape=jax.ShapeDtypeStruct((rows, FIELDS, CHUNK), jnp.bfloat16),
    )(x, weight_in, bias_in, weight_mid, bias_mid, weight_out, bias_out, rate)


def on_device(
    fields,
    zone_ids,
    diffusivity,
    heat_rate,
    weight_in,
    bias_in,
    weight_mid,
    bias_mid,
    weight_out,
    bias_out,
):
    count_here, rows_here, columns = fields.shape
    coefs = lookup(zone_ids, diffusivity)
    stacked = with_halo(jnp.concatenate([fields, coefs], 0), "space", HALO)
    fields_ext = stacked[:count_here]
    coef_pad = pad_rows(stacked[count_here:])
    first_row = lax.axis_index("space") * rows_here - HALO
    global_row = first_row + lax.broadcasted_iota(jnp.int32, (1, rows_here + 2 * HALO, 1), 1)
    inside = (global_row >= 0) & (global_row < rows_here * lax.axis_size("space"))
    state = fields_ext
    for number in range(SWEEPS):
        state = relax_step(pad_rows(state), fields_ext, coef_pad, RELAX_WEIGHTS[number])
        state = jnp.where(inside, state, jnp.float32(0.0))
    state = state[:, HALO : HALO + rows_here]

    chunks = columns // CHUNK
    outgoing = state[0].reshape(rows_here, chunks, CHUNK).transpose(1, 0, 2)
    incoming = lax.all_to_all(outgoing, "field", 0, 0, tiled=True)
    cells = incoming.transpose(1, 0, 2)
    rate = jnp.concatenate([heat_rate, jnp.zeros((FIELDS - heat_rate.shape[0],), jnp.float32)])
    delta = surrogate(
        cells,
        weight_in,
        bias_in[:, None],
        weight_mid,
        bias_mid[:, None],
        weight_out,
        bias_out[:, None],
        rate[:, None],
    )
    returned = lax.all_to_all(delta.transpose(1, 0, 2), "field", 0, 0, tiled=True)
    returned = returned.transpose(1, 0, 2).reshape(1, rows_here, columns)
    return state + returned.astype(jnp.float32)


def solution(mesh):
    return jax.shard_map(
        on_device,
        mesh=mesh,
        in_specs=(
            P("field", "space", None),
            P("space", None),
            P("field", None),
            P(),
            P(),
            P(),
            P(),
            P(),
            P(),
            P(),
        ),
        out_specs=P("field", "space", None),
        check_vma=False,
    )
```

```python
import jax
import jax.numpy as jnp
from jax import lax
from jax.experimental import pallas as pl
from jax.experimental.pallas import tpu as pltpu
from jax.sharding import PartitionSpec as P

FIELDS = 16
SWEEPS = 3
HALO = SWEEPS
CHUNK = 384
ROW_BLOCK = 8

RELAX_WEIGHTS = (0.8, 1.25, 0.95)


def pad_rows(array):
    return jnp.pad(array, ((0, 0), (1, 1), (0, 0)))


def relax_step(padded, source, coef_pad, weight):
    middle = padded[:, 1:-1]
    coef_mid = coef_pad[:, 1:-1]
    face_north = 0.5 * (coef_mid + coef_pad[:, 2:])
    face_south = 0.5 * (coef_mid + coef_pad[:, :-2])
    face_east = 0.5 * (coef_mid + jnp.roll(coef_mid, -1, 2))
    face_west = 0.5 * (coef_mid + jnp.roll(coef_mid, 1, 2))
    diagonal = 1.0 + face_north + face_south + face_east + face_west
    image = diagonal * middle - face_north * padded[:, 2:] - face_south * padded[:, :-2]
    image = image - face_east * jnp.roll(middle, -1, 2) - face_west * jnp.roll(middle, 1, 2)
    return middle + weight * (source - image) / diagonal


def lookup_kernel(table_ref, zone_ref, o_ref):
    zone = zone_ref[...]
    level = [table_ref[0, number] for number in range(table_ref.shape[1])]
    bit = 1
    while len(level) > 1:
        pick = (zone & bit) != 0
        level = [jnp.where(pick, level[k + 1], level[k]) for k in range(0, len(level), 2)]
        bit *= 2
    o_ref[0] = level[0]


def lookup(zone_ids, diffusivity):
    return pl.pallas_call(
        lookup_kernel,
        in_specs=[
            pl.BlockSpec(memory_space=pltpu.SMEM),
            pl.BlockSpec(memory_space=pltpu.VMEM),
        ],
        out_specs=pl.BlockSpec(memory_space=pltpu.VMEM),
        out_shape=jax.ShapeDtypeStruct((1,) + zone_ids.shape, jnp.float32),
    )(diffusivity, zone_ids)


def with_halo(block, axis, width):
    count = lax.axis_size(axis)
    head = block[:, :width]
    tail = block[:, -width:]
    from_above = lax.ppermute(tail, axis, [(i, i + 1) for i in range(count - 1)])
    from_below = lax.ppermute(head, axis, [(i + 1, i) for i in range(count - 1)])
    return jnp.concatenate([from_above, block, from_below], axis=1)


def silu(x):
    half = 0.5 * x
    return half + half * jnp.tanh(half)


def surrogate_kernel(x_ref, w_in_ref, b_in_ref, w_mid_ref, b_mid_ref, w_out_ref, b_out_ref, rate_ref, o_ref):
    w_in = w_in_ref[...]
    w_mid = w_mid_ref[...]
    w_out = w_out_ref[...]
    b_in = b_in_ref[...]
    b_mid = b_mid_ref[...]
    b_out = b_out_ref[...]
    rate = rate_ref[...]
    is_heat = lax.broadcasted_iota(jnp.int32, (FIELDS, CHUNK), 0) == FIELDS - 1

    def row(r, carry):
        x = x_ref[r]
        inputs = x.astype(jnp.bfloat16)
        hidden = silu(jnp.dot(w_in, inputs, preferred_element_type=jnp.float32) + b_in)
        hidden = hidden.astype(jnp.bfloat16)
        hidden = silu(jnp.dot(w_mid, hidden, preferred_element_type=jnp.float32) + b_mid)
        hidden = hidden.astype(jnp.bfloat16)
        change = (jnp.dot(w_out, hidden, preferred_element_type=jnp.float32) + b_out).astype(jnp.bfloat16)
        change = change.astype(jnp.float32)
        heat = x[FIELDS - 1 :] + change[FIELDS - 1 :]
        factor = jnp.exp(rate * jnp.tanh(heat))
        scaled = (change * factor).astype(jnp.bfloat16)
        o_ref[r] = jnp.where(is_heat, change.astype(jnp.bfloat16), scaled)
        return carry

    lax.fori_loop(0, x_ref.shape[0], row, 0)


def surrogate(x, weight_in, bias_in, weight_mid, bias_mid, weight_out, bias_out, rate):
    rows = x.shape[0]
    full = lambda shape: pl.BlockSpec(shape, lambda i: (0,) * len(shape))
    return pl.pallas_call(
        surrogate_kernel,
        grid=(rows // ROW_BLOCK,),
        in_specs=[
            pl.BlockSpec((ROW_BLOCK, FIELDS, CHUNK), lambda i: (i, 0, 0)),
            full(weight_in.shape),
            full(bias_in.shape),
            full(weight_mid.shape),
            full(bias_mid.shape),
            full(weight_out.shape),
            full(bias_out.shape),
            full(rate.shape),
        ],
        out_specs=pl.BlockSpec((ROW_BLOCK, FIELDS, CHUNK), lambda i: (i, 0, 0)),
        out_shape=jax.ShapeDtypeStruct((rows, FIELDS, CHUNK), jnp.bfloat16),
    )(x, weight_in, bias_in, weight_mid, bias_mid, weight_out, bias_out, rate)


def on_device(
    fields,
    zone_ids,
    diffusivity,
    heat_rate,
    weight_in,
    bias_in,
    weight_mid,
    bias_mid,
    weight_out,
    bias_out,
):
    count_here, rows_here, columns = fields.shape
    coefs = lookup(zone_ids, diffusivity)
    stacked = with_halo(jnp.concatenate([fields, coefs], 0), "space", HALO)
    fields_ext = stacked[:count_here]
    coef_pad = pad_rows(stacked[count_here:])
    first_row = lax.axis_index("space") * rows_here - HALO
    global_row = first_row + lax.broadcasted_iota(jnp.int32, (1, rows_here + 2 * HALO, 1), 1)
    inside = (global_row >= 0) & (global_row < rows_here * lax.axis_size("space"))
    state = fields_ext
    for number in range(SWEEPS):
        state = relax_step(pad_rows(state), fields_ext, coef_pad, RELAX_WEIGHTS[number])
        state = jnp.where(inside, state, jnp.float32(0.0))
    state = state[:, HALO : HALO + rows_here]

    chunks = columns // CHUNK
    outgoing = state[0].reshape(rows_here, chunks, CHUNK).transpose(1, 0, 2)
    incoming = lax.all_to_all(outgoing, "field", 0, 0, tiled=True)
    cells = incoming.transpose(1, 0, 2)
    rate = jnp.concatenate([heat_rate, jnp.zeros((FIELDS - heat_rate.shape[0],), jnp.float32)])
    delta = surrogate(
        cells,
        weight_in,
        bias_in[:, None],
        weight_mid,
        bias_mid[:, None],
        weight_out,
        bias_out[:, None],
        rate[:, None],
    )
    returned = lax.all_to_all(delta.transpose(1, 0, 2), "field", 0, 0, tiled=True)
    returned = returned.transpose(1, 0, 2).reshape(1, rows_here, columns)
    return state + returned.astype(jnp.float32)


def solution(mesh):
    return jax.shard_map(
        on_device,
        mesh=mesh,
        in_specs=(
            P("field", "space", None),
            P("space", None),
            P("field", None),
            P(),
            P(),
            P(),
            P(),
            P(),
            P(),
            P(),
        ),
        out_specs=P("field", "space", None),
        check_vma=False,
    )
```

```python
import jax
import jax.numpy as jnp
from jax import lax
from jax.experimental import pallas as pl
from jax.experimental.pallas import tpu as pltpu
from jax.sharding import PartitionSpec as P

FIELDS = 16
SWEEPS = 3
HALO = SWEEPS
CHUNK = 384

RELAX_WEIGHTS = (0.8, 1.25, 0.95)


def pad_rows(array):
    return jnp.pad(array, ((0, 0), (1, 1), (0, 0)))


def relax_step(padded, source, coef_pad, weight):
    middle = padded[:, 1:-1]
    coef_mid = coef_pad[:, 1:-1]
    face_north = 0.5 * (coef_mid + coef_pad[:, 2:])
    face_south = 0.5 * (coef_mid + coef_pad[:, :-2])
    face_east = 0.5 * (coef_mid + jnp.roll(coef_mid, -1, 2))
    face_west = 0.5 * (coef_mid + jnp.roll(coef_mid, 1, 2))
    diagonal = 1.0 + face_north + face_south + face_east + face_west
    image = diagonal * middle - face_north * padded[:, 2:] - face_south * padded[:, :-2]
    image = image - face_east * jnp.roll(middle, -1, 2) - face_west * jnp.roll(middle, 1, 2)
    return middle + weight * (source - image) / diagonal


def lookup_kernel(table_ref, zone_ref, o_ref):
    zone = zone_ref[...]
    level = [table_ref[0, number] for number in range(table_ref.shape[1])]
    bit = 1
    while len(level) > 1:
        pick = (zone & bit) != 0
        level = [jnp.where(pick, level[k + 1], level[k]) for k in range(0, len(level), 2)]
        bit *= 2
    o_ref[0] = level[0]


def lookup(zone_ids, diffusivity):
    return pl.pallas_call(
        lookup_kernel,
        in_specs=[
            pl.BlockSpec(memory_space=pltpu.SMEM),
            pl.BlockSpec(memory_space=pltpu.VMEM),
        ],
        out_specs=pl.BlockSpec(memory_space=pltpu.VMEM),
        out_shape=jax.ShapeDtypeStruct((1,) + zone_ids.shape, jnp.float32),
    )(diffusivity, zone_ids)


def with_halo(block, axis, width):
    count = lax.axis_size(axis)
    head = block[:, :width]
    tail = block[:, -width:]
    from_above = lax.ppermute(tail, axis, [(i, i + 1) for i in range(count - 1)])
    from_below = lax.ppermute(head, axis, [(i + 1, i) for i in range(count - 1)])
    return jnp.concatenate([from_above, block, from_below], axis=1)


def surrogate(cells, weight_in, bias_in, weight_mid, bias_mid, weight_out, bias_out, rate):
    inputs = cells.astype(jnp.bfloat16)
    hidden = jax.nn.silu(
        jnp.dot(weight_in, inputs, preferred_element_type=jnp.float32) + bias_in[:, None]
    ).astype(jnp.bfloat16)
    hidden = jax.nn.silu(
        jnp.dot(weight_mid, hidden, preferred_element_type=jnp.float32) + bias_mid[:, None]
    ).astype(jnp.bfloat16)
    change = (jnp.dot(weight_out, hidden, preferred_element_type=jnp.float32) + bias_out[:, None]).astype(
        jnp.bfloat16
    )
    heat = cells[-1] + change[-1].astype(jnp.float32)
    factor = jnp.exp(rate[:, None] * jnp.tanh(heat)[None])
    scaled = (change[:-1].astype(jnp.float32) * factor).astype(jnp.bfloat16)
    return jnp.concatenate([scaled, change[-1:]], 0)


def on_device(
    fields,
    zone_ids,
    diffusivity,
    heat_rate,
    weight_in,
    bias_in,
    weight_mid,
    bias_mid,
    weight_out,
    bias_out,
):
    count_here, rows_here, columns = fields.shape
    coefs = lookup(zone_ids, diffusivity)
    stacked = with_halo(jnp.concatenate([fields, coefs], 0), "space", HALO)
    fields_ext = stacked[:count_here]
    coef_pad = pad_rows(stacked[count_here:])
    first_row = lax.axis_index("space") * rows_here - HALO
    global_row = first_row + lax.broadcasted_iota(jnp.int32, (1, rows_here + 2 * HALO, 1), 1)
    inside = (global_row >= 0) & (global_row < rows_here * lax.axis_size("space"))
    state = fields_ext
    for number in range(SWEEPS):
        state = relax_step(pad_rows(state), fields_ext, coef_pad, RELAX_WEIGHTS[number])
        state = jnp.where(inside, state, jnp.float32(0.0))
    state = state[:, HALO : HALO + rows_here]

    chunks = columns // CHUNK
    outgoing = state[0].reshape(rows_here, chunks, CHUNK).transpose(1, 0, 2)
    incoming = lax.all_to_all(outgoing, "field", 0, 0, tiled=True)
    delta = surrogate(
        incoming.reshape(FIELDS, rows_here * CHUNK),
        weight_in,
        bias_in,
        weight_mid,
        bias_mid,
        weight_out,
        bias_out,
        heat_rate,
    )
    returned = lax.all_to_all(delta.reshape(FIELDS, rows_here, CHUNK), "field", 0, 0, tiled=True)
    returned = returned.transpose(1, 0, 2).reshape(1, rows_here, columns)
    return state + returned.astype(jnp.float32)


def solution(mesh):
    return jax.shard_map(
        on_device,
        mesh=mesh,
        in_specs=(
            P("field", "space", None),
            P("space", None),
            P("field", None),
            P(),
            P(),
            P(),
            P(),
            P(),
            P(),
            P(),
        ),
        out_specs=P("field", "space", None),
        check_vma=False,
    )
```

```python
import jax
import jax.numpy as jnp
from jax import lax
from jax.experimental import pallas as pl
from jax.experimental.pallas import tpu as pltpu
from jax.sharding import PartitionSpec as P

FIELDS = 16
SWEEPS = 3
HALO = SWEEPS
CHUNK = 384

RELAX_WEIGHTS = (0.8, 1.25, 0.95)


def pad_rows(array):
    return jnp.pad(array, ((0, 0), (1, 1), (0, 0)))


def relax_step(padded, source, coef_pad, weight):
    middle = padded[:, 1:-1]
    coef_mid = coef_pad[:, 1:-1]
    face_north = 0.5 * (coef_mid + coef_pad[:, 2:])
    face_south = 0.5 * (coef_mid + coef_pad[:, :-2])
    face_east = 0.5 * (coef_mid + jnp.roll(coef_mid, -1, 2))
    face_west = 0.5 * (coef_mid + jnp.roll(coef_mid, 1, 2))
    diagonal = 1.0 + face_north + face_south + face_east + face_west
    image = diagonal * middle - face_north * padded[:, 2:] - face_south * padded[:, :-2]
    image = image - face_east * jnp.roll(middle, -1, 2) - face_west * jnp.roll(middle, 1, 2)
    return middle + weight * (source - image) / diagonal


def lookup_kernel(table_ref, zone_ref, o_ref):
    zone = zone_ref[...]
    level = [table_ref[0, number] for number in range(table_ref.shape[1])]
    bit = 1
    while len(level) > 1:
        pick = (zone & bit) != 0
        level = [jnp.where(pick, level[k + 1], level[k]) for k in range(0, len(level), 2)]
        bit *= 2
    o_ref[0] = level[0]


def lookup(zone_ids, diffusivity):
    return pl.pallas_call(
        lookup_kernel,
        in_specs=[
            pl.BlockSpec(memory_space=pltpu.SMEM),
            pl.BlockSpec(memory_space=pltpu.VMEM),
        ],
        out_specs=pl.BlockSpec(memory_space=pltpu.VMEM),
        out_shape=jax.ShapeDtypeStruct((1,) + zone_ids.shape, jnp.float32),
    )(diffusivity, zone_ids)


def select_tree(zone, table):
    level = [table[number] for number in range(table.shape[0])]
    bit = 1
    while len(level) > 1:
        pick = (zone & bit) != 0
        level = [jnp.where(pick, level[k + 1], level[k]) for k in range(0, len(level), 2)]
        bit *= 2
    return level[0]


def sweeps(source, coef, inside):
    coef_pad = pad_rows(coef)
    state = source
    for number in range(SWEEPS):
        state = relax_step(pad_rows(state), source, coef_pad, RELAX_WEIGHTS[number])
        if inside is not None:
            state = jnp.where(inside, state, jnp.float32(0.0))
    return state


def surrogate(cells, weight_in, bias_in, weight_mid, bias_mid, weight_out, bias_out, rate):
    inputs = cells.astype(jnp.bfloat16)
    hidden = jax.nn.silu(
        jnp.dot(weight_in, inputs, preferred_element_type=jnp.float32) + bias_in[:, None]
    ).astype(jnp.bfloat16)
    hidden = jax.nn.silu(
        jnp.dot(weight_mid, hidden, preferred_element_type=jnp.float32) + bias_mid[:, None]
    ).astype(jnp.bfloat16)
    change = (jnp.dot(weight_out, hidden, preferred_element_type=jnp.float32) + bias_out[:, None]).astype(
        jnp.bfloat16
    )
    heat = cells[-1] + change[-1].astype(jnp.float32)
    factor = jnp.exp(rate[:, None] * jnp.tanh(heat)[None])
    scaled = (change[:-1].astype(jnp.float32) * factor).astype(jnp.bfloat16)
    return jnp.concatenate([scaled, change[-1:]], 0)


def on_device(
    fields,
    zone_ids,
    diffusivity,
    heat_rate,
    weight_in,
    bias_in,
    weight_mid,
    bias_mid,
    weight_out,
    bias_out,
):
    count_here, rows_here, columns = fields.shape
    count = lax.axis_size("space")
    raw = jnp.concatenate([fields, zone_ids.astype(jnp.float32)[None]], 0)
    from_above = lax.ppermute(raw[:, -HALO:], "space", [(i, i + 1) for i in range(count - 1)])
    from_below = lax.ppermute(raw[:, :HALO], "space", [(i + 1, i) for i in range(count - 1)])
    coefs = lookup(zone_ids, diffusivity)
    interior = sweeps(fields, coefs, None)
    strip = 3 * HALO
    first_row = lax.axis_index("space") * rows_here
    offsets = jnp.array([-HALO, rows_here - 2 * HALO], jnp.int32)[:, None, None]
    global_row = first_row + offsets + lax.broadcasted_iota(jnp.int32, (2, strip, 1), 1)
    inside = (global_row >= 0) & (global_row < rows_here * count)
    halo = jnp.stack([from_above, from_below])
    halo_fields = halo[:, 0]
    halo_coef = select_tree(halo[:, 1].astype(jnp.int32), diffusivity[0])
    strip_fields = jnp.stack(
        [
            jnp.concatenate([halo_fields[0], fields[0, : 2 * HALO]], 0),
            jnp.concatenate([fields[0, -2 * HALO :], halo_fields[1]], 0),
        ]
    )
    strip_coef = jnp.stack(
        [
            jnp.concatenate([halo_coef[0], coefs[0, : 2 * HALO]], 0),
            jnp.concatenate([coefs[0, -2 * HALO :], halo_coef[1]], 0),
        ]
    )
    strip_coef = jnp.where(inside, strip_coef, jnp.float32(0.0))
    edges = sweeps(strip_fields, strip_coef, inside)
    state = jnp.concatenate(
        [edges[0, HALO : 2 * HALO], interior[0, HALO : rows_here - HALO], edges[1, HALO : 2 * HALO]], 0
    )[None]

    chunks = columns // CHUNK
    outgoing = state[0].reshape(rows_here, chunks, CHUNK).transpose(1, 0, 2)
    incoming = lax.all_to_all(outgoing, "field", 0, 0, tiled=True)
    delta = surrogate(
        incoming.reshape(FIELDS, rows_here * CHUNK),
        weight_in,
        bias_in,
        weight_mid,
        bias_mid,
        weight_out,
        bias_out,
        heat_rate,
    )
    returned = lax.all_to_all(delta.reshape(FIELDS, rows_here, CHUNK), "field", 0, 0, tiled=True)
    returned = returned.transpose(1, 0, 2).reshape(1, rows_here, columns)
    return state + returned.astype(jnp.float32)


def solution(mesh):
    return jax.shard_map(
        on_device,
        mesh=mesh,
        in_specs=(
            P("field", "space", None),
            P("space", None),
            P("field", None),
            P(),
            P(),
            P(),
            P(),
            P(),
            P(),
            P(),
        ),
        out_specs=P("field", "space", None),
        check_vma=False,
    )
```

```python
import jax
import jax.numpy as jnp
from jax import lax
from jax.experimental import pallas as pl
from jax.experimental.pallas import tpu as pltpu
from jax.sharding import PartitionSpec as P

FIELDS = 16
SWEEPS = 3
HALO = SWEEPS
ROOM = 8
CHUNK = 384

RELAX_WEIGHTS = (0.8, 1.25, 0.95)


def pad_rows(array):
    return jnp.pad(array, ((0, 0), (1, 1), (0, 0)))


def relax_step(padded, source, coef_pad, weight):
    middle = padded[:, 1:-1]
    coef_mid = coef_pad[:, 1:-1]
    face_north = 0.5 * (coef_mid + coef_pad[:, 2:])
    face_south = 0.5 * (coef_mid + coef_pad[:, :-2])
    face_east = 0.5 * (coef_mid + jnp.roll(coef_mid, -1, 2))
    face_west = 0.5 * (coef_mid + jnp.roll(coef_mid, 1, 2))
    diagonal = 1.0 + face_north + face_south + face_east + face_west
    image = diagonal * middle - face_north * padded[:, 2:] - face_south * padded[:, :-2]
    image = image - face_east * jnp.roll(middle, -1, 2) - face_west * jnp.roll(middle, 1, 2)
    return middle + weight * (source - image) / diagonal


def lookup_kernel(table_ref, zone_ref, o_ref):
    zone = zone_ref[...]
    level = [table_ref[0, number] for number in range(table_ref.shape[1])]
    bit = 1
    while len(level) > 1:
        pick = (zone & bit) != 0
        level = [jnp.where(pick, level[k + 1], level[k]) for k in range(0, len(level), 2)]
        bit *= 2
    o_ref[0] = level[0]


def lookup(zone_ids, diffusivity):
    return pl.pallas_call(
        lookup_kernel,
        in_specs=[
            pl.BlockSpec(memory_space=pltpu.SMEM),
            pl.BlockSpec(memory_space=pltpu.VMEM),
        ],
        out_specs=pl.BlockSpec(memory_space=pltpu.VMEM),
        out_shape=jax.ShapeDtypeStruct((1,) + zone_ids.shape, jnp.float32),
    )(diffusivity, zone_ids)


def with_halo(block, axis, width, room):
    count = lax.axis_size(axis)
    head = block[:, :width]
    tail = block[:, -width:]
    from_above = lax.ppermute(tail, axis, [(i, i + 1) for i in range(count - 1)])
    from_below = lax.ppermute(head, axis, [(i + 1, i) for i in range(count - 1)])
    zeros = jnp.zeros(block.shape[:1] + (room - width,) + block.shape[2:], block.dtype)
    return jnp.concatenate([zeros, from_above, block, from_below, zeros], axis=1)


def diffusion_kernel(bounds_ref, ext_ref, state_ref, chunks_ref):
    _, rows, cols = ext_ref.shape
    here = state_ref.shape[1]
    q = lax.broadcasted_iota(jnp.int32, (rows, cols), 0)
    inside = (q >= bounds_ref[0]) & (q < bounds_ref[1])
    coef = ext_ref[1]
    face_north = 0.5 * (coef + pltpu.roll(coef, rows - 1, 0))
    face_south = 0.5 * (coef + pltpu.roll(coef, 1, 0))
    face_east = 0.5 * (coef + pltpu.roll(coef, cols - 1, 1))
    face_west = 0.5 * (coef + pltpu.roll(coef, 1, 1))
    diagonal = 1.0 + face_north + face_south + face_east + face_west
    source = ext_ref[0]
    state = source
    for weight in RELAX_WEIGHTS:
        image = (
            diagonal * state
            - face_north * pltpu.roll(state, rows - 1, 0)
            - face_south * pltpu.roll(state, 1, 0)
        )
        image = image - face_east * pltpu.roll(state, cols - 1, 1) - face_west * pltpu.roll(state, 1, 1)
        state = state + weight * (source - image) / diagonal
        state = jnp.where(inside, state, jnp.float32(0.0))
    state = state[ROOM : ROOM + here]
    state_ref[0] = state
    for number in range(chunks_ref.shape[0]):
        chunks_ref[number] = state[:, number * CHUNK : (number + 1) * CHUNK]


def diffusion(ext, bounds, here):
    _, rows, cols = ext.shape
    return pl.pallas_call(
        diffusion_kernel,
        in_specs=[
            pl.BlockSpec(memory_space=pltpu.SMEM),
            pl.BlockSpec(memory_space=pltpu.VMEM),
        ],
        out_specs=[
            pl.BlockSpec(memory_space=pltpu.VMEM),
            pl.BlockSpec(memory_space=pltpu.VMEM),
        ],
        out_shape=[
            jax.ShapeDtypeStruct((1, here, cols), jnp.float32),
            jax.ShapeDtypeStruct((cols // CHUNK, here, CHUNK), jnp.float32),
        ],
    )(bounds, ext)


def surrogate(cells, weight_in, bias_in, weight_mid, bias_mid, weight_out, bias_out, rate):
    inputs = cells.astype(jnp.bfloat16)
    hidden = jax.nn.silu(
        jnp.dot(weight_in, inputs, preferred_element_type=jnp.float32) + bias_in[:, None]
    ).astype(jnp.bfloat16)
    hidden = jax.nn.silu(
        jnp.dot(weight_mid, hidden, preferred_element_type=jnp.float32) + bias_mid[:, None]
    ).astype(jnp.bfloat16)
    change = (jnp.dot(weight_out, hidden, preferred_element_type=jnp.float32) + bias_out[:, None]).astype(
        jnp.bfloat16
    )
    heat = cells[-1] + change[-1].astype(jnp.float32)
    factor = jnp.exp(rate[:, None] * jnp.tanh(heat)[None])
    scaled = (change[:-1].astype(jnp.float32) * factor).astype(jnp.bfloat16)
    return jnp.concatenate([scaled, change[-1:]], 0)


def on_device(
    fields,
    zone_ids,
    diffusivity,
    heat_rate,
    weight_in,
    bias_in,
    weight_mid,
    bias_mid,
    weight_out,
    bias_out,
):
    count_here, rows_here, columns = fields.shape
    coefs = lookup(zone_ids, diffusivity)
    ext = with_halo(jnp.concatenate([fields, coefs], 0), "space", HALO, ROOM)
    first = ROOM - lax.axis_index("space") * rows_here
    bounds = jnp.stack(
        [
            jnp.maximum(ROOM - HALO, first),
            jnp.minimum(ROOM + rows_here + HALO, first + rows_here * lax.axis_size("space")),
        ]
    ).astype(jnp.int32)
    state, outgoing = diffusion(ext, bounds, rows_here)
    incoming = lax.all_to_all(outgoing, "field", 0, 0, tiled=True)
    delta = surrogate(
        incoming.reshape(FIELDS, rows_here * CHUNK),
        weight_in,
        bias_in,
        weight_mid,
        bias_mid,
        weight_out,
        bias_out,
        heat_rate,
    )
    returned = lax.all_to_all(delta.reshape(FIELDS, rows_here, CHUNK), "field", 0, 0, tiled=True)
    returned = returned.transpose(1, 0, 2).reshape(1, rows_here, columns)
    return state + returned.astype(jnp.float32)


def solution(mesh):
    return jax.shard_map(
        on_device,
        mesh=mesh,
        in_specs=(
            P("field", "space", None),
            P("space", None),
            P("field", None),
            P(),
            P(),
            P(),
            P(),
            P(),
            P(),
            P(),
        ),
        out_specs=P("field", "space", None),
        check_vma=False,
    )
```

```python
import jax
import jax.numpy as jnp
from jax import lax
from jax.experimental import pallas as pl
from jax.experimental.pallas import tpu as pltpu
from jax.sharding import PartitionSpec as P

FIELDS = 16
SWEEPS = 3
HALO = SWEEPS
CHUNK = 384
ROW_BLOCK = 8
NT = (((1,), (1,)), ((), ()))

RELAX_WEIGHTS = (0.8, 1.25, 0.95)


def pad_rows(array):
    return jnp.pad(array, ((0, 0), (1, 1), (0, 0)))


def relax_step(padded, source, coef_pad, weight):
    middle = padded[:, 1:-1]
    coef_mid = coef_pad[:, 1:-1]
    face_north = 0.5 * (coef_mid + coef_pad[:, 2:])
    face_south = 0.5 * (coef_mid + coef_pad[:, :-2])
    face_east = 0.5 * (coef_mid + jnp.roll(coef_mid, -1, 2))
    face_west = 0.5 * (coef_mid + jnp.roll(coef_mid, 1, 2))
    diagonal = 1.0 + face_north + face_south + face_east + face_west
    image = diagonal * middle - face_north * padded[:, 2:] - face_south * padded[:, :-2]
    image = image - face_east * jnp.roll(middle, -1, 2) - face_west * jnp.roll(middle, 1, 2)
    return middle + weight * (source - image) / diagonal


def lookup_kernel(table_ref, zone_ref, o_ref):
    zone = zone_ref[...]
    level = [table_ref[0, number] for number in range(table_ref.shape[1])]
    bit = 1
    while len(level) > 1:
        pick = (zone & bit) != 0
        level = [jnp.where(pick, level[k + 1], level[k]) for k in range(0, len(level), 2)]
        bit *= 2
    o_ref[0] = level[0]


def lookup(zone_ids, diffusivity):
    return pl.pallas_call(
        lookup_kernel,
        in_specs=[
            pl.BlockSpec(memory_space=pltpu.SMEM),
            pl.BlockSpec(memory_space=pltpu.VMEM),
        ],
        out_specs=pl.BlockSpec(memory_space=pltpu.VMEM),
        out_shape=jax.ShapeDtypeStruct((1,) + zone_ids.shape, jnp.float32),
    )(diffusivity, zone_ids)


def with_halo(block, axis, width):
    count = lax.axis_size(axis)
    head = block[:, :width]
    tail = block[:, -width:]
    from_above = lax.ppermute(tail, axis, [(i, i + 1) for i in range(count - 1)])
    from_below = lax.ppermute(head, axis, [(i + 1, i) for i in range(count - 1)])
    return jnp.concatenate([from_above, block, from_below], axis=1)


def mlp_kernel(x_ref, w_in_ref, b_in_ref, w_mid_ref, b_mid_ref, w_out_ref, b_out_ref, rate_ref, o_ref):
    rows = x_ref.shape[0]
    cells = jnp.concatenate([x_ref[r].T for r in range(rows)], axis=0)
    inputs = cells.astype(jnp.bfloat16)
    hidden = jax.nn.silu(lax.dot_general(inputs, w_in_ref[...], NT, preferred_element_type=jnp.float32) + b_in_ref[...])
    hidden = hidden.astype(jnp.bfloat16)
    hidden = jax.nn.silu(lax.dot_general(hidden, w_mid_ref[...], NT, preferred_element_type=jnp.float32) + b_mid_ref[...])
    hidden = hidden.astype(jnp.bfloat16)
    change = lax.dot_general(hidden, w_out_ref[...], NT, preferred_element_type=jnp.float32) + b_out_ref[...]
    change = change.astype(jnp.bfloat16).astype(jnp.float32).T
    x = cells.T
    heat = x[FIELDS - 1 :] + change[FIELDS - 1 :]
    factor = jnp.exp(rate_ref[...] * jnp.tanh(heat))
    scaled = (change * factor).astype(jnp.bfloat16)
    is_heat = lax.broadcasted_iota(jnp.int32, change.shape, 0) == FIELDS - 1
    out = jnp.where(is_heat, change.astype(jnp.bfloat16), scaled)
    for r in range(rows):
        o_ref[r] = out[:, r * CHUNK : (r + 1) * CHUNK]

def surrogate_rows(x, weight_in, bias_in, weight_mid, bias_mid, weight_out, bias_out, rate):
    rows = x.shape[0]
    full = lambda shape: pl.BlockSpec(shape, lambda i: (0,) * len(shape))
    return pl.pallas_call(
        mlp_kernel,
        grid=(rows // ROW_BLOCK,),
        in_specs=[pl.BlockSpec((ROW_BLOCK, FIELDS, CHUNK), lambda i: (i, 0, 0)),
                  full(weight_in.shape), full(bias_in.shape), full(weight_mid.shape), full(bias_mid.shape),
                  full(weight_out.shape), full(bias_out.shape), full(rate.shape)],
        out_specs=pl.BlockSpec((ROW_BLOCK, FIELDS, CHUNK), lambda i: (i, 0, 0)),
        out_shape=jax.ShapeDtypeStruct((rows, FIELDS, CHUNK), jnp.bfloat16),
    )(x, weight_in, bias_in, weight_mid, bias_mid, weight_out, bias_out, rate)


def on_device(
    fields,
    zone_ids,
    diffusivity,
    heat_rate,
    weight_in,
    bias_in,
    weight_mid,
    bias_mid,
    weight_out,
    bias_out,
):
    count_here, rows_here, columns = fields.shape
    coefs = lookup(zone_ids, diffusivity)
    stacked = with_halo(jnp.concatenate([fields, coefs], 0), "space", HALO)
    fields_ext = stacked[:count_here]
    coef_pad = pad_rows(stacked[count_here:])
    first_row = lax.axis_index("space") * rows_here - HALO
    global_row = first_row + lax.broadcasted_iota(jnp.int32, (1, rows_here + 2 * HALO, 1), 1)
    inside = (global_row >= 0) & (global_row < rows_here * lax.axis_size("space"))
    state = fields_ext
    for number in range(SWEEPS):
        state = relax_step(pad_rows(state), fields_ext, coef_pad, RELAX_WEIGHTS[number])
        state = jnp.where(inside, state, jnp.float32(0.0))
    state = state[:, HALO : HALO + rows_here]

    chunks = columns // CHUNK
    outgoing = state[0].reshape(rows_here, chunks, CHUNK).transpose(1, 0, 2)
    incoming = lax.all_to_all(outgoing, "field", 0, 0, tiled=True)
    rate = jnp.concatenate([heat_rate, jnp.zeros((FIELDS - heat_rate.shape[0],), jnp.float32)])
    delta = surrogate_rows(
        incoming.transpose(1, 0, 2),
        weight_in,
        bias_in[None],
        weight_mid,
        bias_mid[None],
        weight_out,
        bias_out[None],
        rate[:, None],
    )
    returned = lax.all_to_all(delta.transpose(1, 0, 2), "field", 0, 0, tiled=True)
    returned = returned.transpose(1, 0, 2).reshape(1, rows_here, columns)
    return state + returned.astype(jnp.float32)


def solution(mesh):
    return jax.shard_map(
        on_device,
        mesh=mesh,
        in_specs=(
            P("field", "space", None),
            P("space", None),
            P("field", None),
            P(),
            P(),
            P(),
            P(),
            P(),
            P(),
            P(),
        ),
        out_specs=P("field", "space", None),
        check_vma=False,
    )
```

```python
import jax
import jax.numpy as jnp
from jax import lax
from jax.experimental import pallas as pl
from jax.experimental.pallas import tpu as pltpu
from jax.sharding import PartitionSpec as P

FIELDS = 16
SWEEPS = 3
HALO = SWEEPS
CHUNK = 384
ROW_BLOCK = 8
GROUPS = 2
NT = (((1,), (1,)), ((), ()))

RELAX_WEIGHTS = (0.8, 1.25, 0.95)


def pad_rows(array):
    return jnp.pad(array, ((0, 0), (1, 1), (0, 0)))


def relax_step(padded, source, coef_pad, weight):
    middle = padded[:, 1:-1]
    coef_mid = coef_pad[:, 1:-1]
    face_north = 0.5 * (coef_mid + coef_pad[:, 2:])
    face_south = 0.5 * (coef_mid + coef_pad[:, :-2])
    face_east = 0.5 * (coef_mid + jnp.roll(coef_mid, -1, 2))
    face_west = 0.5 * (coef_mid + jnp.roll(coef_mid, 1, 2))
    diagonal = 1.0 + face_north + face_south + face_east + face_west
    image = diagonal * middle - face_north * padded[:, 2:] - face_south * padded[:, :-2]
    image = image - face_east * jnp.roll(middle, -1, 2) - face_west * jnp.roll(middle, 1, 2)
    return middle + weight * (source - image) / diagonal


def lookup_kernel(table_ref, zone_ref, o_ref):
    zone = zone_ref[...]
    level = [table_ref[0, number] for number in range(table_ref.shape[1])]
    bit = 1
    while len(level) > 1:
        pick = (zone & bit) != 0
        level = [jnp.where(pick, level[k + 1], level[k]) for k in range(0, len(level), 2)]
        bit *= 2
    o_ref[0] = level[0]


def lookup(zone_ids, diffusivity):
    return pl.pallas_call(
        lookup_kernel,
        in_specs=[
            pl.BlockSpec(memory_space=pltpu.SMEM),
            pl.BlockSpec(memory_space=pltpu.VMEM),
        ],
        out_specs=pl.BlockSpec(memory_space=pltpu.VMEM),
        out_shape=jax.ShapeDtypeStruct((1,) + zone_ids.shape, jnp.float32),
    )(diffusivity, zone_ids)


def with_halo(block, axis, width):
    count = lax.axis_size(axis)
    head = block[:, :width]
    tail = block[:, -width:]
    from_above = lax.ppermute(tail, axis, [(i, i + 1) for i in range(count - 1)])
    from_below = lax.ppermute(head, axis, [(i + 1, i) for i in range(count - 1)])
    return jnp.concatenate([from_above, block, from_below], axis=1)


def mlp_kernel(x_ref, w_in_ref, b_in_ref, w_mid_ref, b_mid_ref, w_out_ref, b_out_ref, rate_ref, o_ref):
    rows = x_ref.shape[0]
    cells = jnp.concatenate([x_ref[r].T for r in range(rows)], axis=0)
    inputs = cells.astype(jnp.bfloat16)
    hidden = jax.nn.silu(lax.dot_general(inputs, w_in_ref[...], NT, preferred_element_type=jnp.float32) + b_in_ref[...])
    hidden = hidden.astype(jnp.bfloat16)
    hidden = jax.nn.silu(lax.dot_general(hidden, w_mid_ref[...], NT, preferred_element_type=jnp.float32) + b_mid_ref[...])
    hidden = hidden.astype(jnp.bfloat16)
    change = lax.dot_general(hidden, w_out_ref[...], NT, preferred_element_type=jnp.float32) + b_out_ref[...]
    change = change.astype(jnp.bfloat16).astype(jnp.float32).T
    x = cells.T
    heat = x[FIELDS - 1 :] + change[FIELDS - 1 :]
    factor = jnp.exp(rate_ref[...] * jnp.tanh(heat))
    scaled = (change * factor).astype(jnp.bfloat16)
    is_heat = lax.broadcasted_iota(jnp.int32, change.shape, 0) == FIELDS - 1
    out = jnp.where(is_heat, change.astype(jnp.bfloat16), scaled)
    for r in range(rows):
        o_ref[r] = out[:, r * CHUNK : (r + 1) * CHUNK]

def surrogate_rows(x, weight_in, bias_in, weight_mid, bias_mid, weight_out, bias_out, rate):
    rows = x.shape[0]
    full = lambda shape: pl.BlockSpec(shape, lambda i: (0,) * len(shape))
    return pl.pallas_call(
        mlp_kernel,
        grid=(rows // ROW_BLOCK,),
        in_specs=[pl.BlockSpec((ROW_BLOCK, FIELDS, CHUNK), lambda i: (i, 0, 0)),
                  full(weight_in.shape), full(bias_in.shape), full(weight_mid.shape), full(bias_mid.shape),
                  full(weight_out.shape), full(bias_out.shape), full(rate.shape)],
        out_specs=pl.BlockSpec((ROW_BLOCK, FIELDS, CHUNK), lambda i: (i, 0, 0)),
        out_shape=jax.ShapeDtypeStruct((rows, FIELDS, CHUNK), jnp.bfloat16),
    )(x, weight_in, bias_in, weight_mid, bias_mid, weight_out, bias_out, rate)


def on_device(
    fields,
    zone_ids,
    diffusivity,
    heat_rate,
    weight_in,
    bias_in,
    weight_mid,
    bias_mid,
    weight_out,
    bias_out,
):
    count_here, rows_here, columns = fields.shape
    coefs = lookup(zone_ids, diffusivity)
    stacked = with_halo(jnp.concatenate([fields, coefs], 0), "space", HALO)
    fields_ext = stacked[:count_here]
    coef_pad = pad_rows(stacked[count_here:])
    first_row = lax.axis_index("space") * rows_here - HALO
    global_row = first_row + lax.broadcasted_iota(jnp.int32, (1, rows_here + 2 * HALO, 1), 1)
    inside = (global_row >= 0) & (global_row < rows_here * lax.axis_size("space"))
    state = fields_ext
    for number in range(SWEEPS):
        state = relax_step(pad_rows(state), fields_ext, coef_pad, RELAX_WEIGHTS[number])
        state = jnp.where(inside, state, jnp.float32(0.0))
    state = state[:, HALO : HALO + rows_here]

    chunks = columns // CHUNK
    rate = jnp.concatenate([heat_rate, jnp.zeros((FIELDS - heat_rate.shape[0],), jnp.float32)])
    group = rows_here // GROUPS
    pieces = []
    for number in range(GROUPS):
        part = state[0, number * group : (number + 1) * group]
        outgoing = part.reshape(group, chunks, CHUNK).transpose(1, 0, 2)
        incoming = lax.all_to_all(outgoing, "field", 0, 0, tiled=True)
        delta = surrogate_rows(
            incoming.transpose(1, 0, 2),
            weight_in,
            bias_in[None],
            weight_mid,
            bias_mid[None],
            weight_out,
            bias_out[None],
            rate[:, None],
        )
        returned = lax.all_to_all(delta.transpose(1, 0, 2), "field", 0, 0, tiled=True)
        returned = returned.transpose(1, 0, 2).reshape(group, columns)
        pieces.append(part + returned.astype(jnp.float32))
    return jnp.concatenate(pieces, 0)[None]


def solution(mesh):
    return jax.shard_map(
        on_device,
        mesh=mesh,
        in_specs=(
            P("field", "space", None),
            P("space", None),
            P("field", None),
            P(),
            P(),
            P(),
            P(),
            P(),
            P(),
            P(),
        ),
        out_specs=P("field", "space", None),
        check_vma=False,
    )
```

```python
import jax
import jax.numpy as jnp
from jax import lax
from jax.experimental import pallas as pl
from jax.experimental.pallas import tpu as pltpu
from jax.sharding import PartitionSpec as P

FIELDS = 16
SWEEPS = 3
HALO = SWEEPS
CHUNK = 384
ROW_BLOCK = 8
NT = (((1,), (1,)), ((), ()))

RELAX_WEIGHTS = (0.8, 1.25, 0.95)


def pad_rows(array):
    return jnp.pad(array, ((0, 0), (1, 1), (0, 0)))


def relax_step(padded, source, coef_pad, weight):
    middle = padded[:, 1:-1]
    coef_mid = coef_pad[:, 1:-1]
    face_north = 0.5 * (coef_mid + coef_pad[:, 2:])
    face_south = 0.5 * (coef_mid + coef_pad[:, :-2])
    face_east = 0.5 * (coef_mid + jnp.roll(coef_mid, -1, 2))
    face_west = 0.5 * (coef_mid + jnp.roll(coef_mid, 1, 2))
    diagonal = 1.0 + face_north + face_south + face_east + face_west
    image = diagonal * middle - face_north * padded[:, 2:] - face_south * padded[:, :-2]
    image = image - face_east * jnp.roll(middle, -1, 2) - face_west * jnp.roll(middle, 1, 2)
    return middle + weight * (source - image) / diagonal


def lookup_kernel(table_ref, zone_ref, o_ref):
    zone = zone_ref[...]
    level = [table_ref[0, number] for number in range(table_ref.shape[1])]
    bit = 1
    while len(level) > 1:
        pick = (zone & bit) != 0
        level = [jnp.where(pick, level[k + 1], level[k]) for k in range(0, len(level), 2)]
        bit *= 2
    o_ref[0] = level[0]


def lookup(zone_ids, diffusivity):
    return pl.pallas_call(
        lookup_kernel,
        in_specs=[
            pl.BlockSpec(memory_space=pltpu.SMEM),
            pl.BlockSpec(memory_space=pltpu.VMEM),
        ],
        out_specs=pl.BlockSpec(memory_space=pltpu.VMEM),
        out_shape=jax.ShapeDtypeStruct((1,) + zone_ids.shape, jnp.float32),
    )(diffusivity, zone_ids)


def with_halo(block, axis, width):
    count = lax.axis_size(axis)
    head = block[:, :width]
    tail = block[:, -width:]
    from_above = lax.ppermute(tail, axis, [(i, i + 1) for i in range(count - 1)])
    from_below = lax.ppermute(head, axis, [(i + 1, i) for i in range(count - 1)])
    return jnp.concatenate([from_above, block, from_below], axis=1)


def mlp_kernel(x_ref, w_in_ref, b_in_ref, w_mid_ref, b_mid_ref, w_out_ref, b_out_ref, rate_ref, o_ref):
    rows = x_ref.shape[0]
    cells = jnp.concatenate([x_ref[r].astype(jnp.float32).T for r in range(rows)], axis=0)
    inputs = cells.astype(jnp.bfloat16)
    hidden = jax.nn.silu(lax.dot_general(inputs, w_in_ref[...], NT, preferred_element_type=jnp.float32) + b_in_ref[...])
    hidden = hidden.astype(jnp.bfloat16)
    hidden = jax.nn.silu(lax.dot_general(hidden, w_mid_ref[...], NT, preferred_element_type=jnp.float32) + b_mid_ref[...])
    hidden = hidden.astype(jnp.bfloat16)
    change = lax.dot_general(hidden, w_out_ref[...], NT, preferred_element_type=jnp.float32) + b_out_ref[...]
    change = change.astype(jnp.bfloat16).astype(jnp.float32).T
    x = cells.T
    heat = x[FIELDS - 1 :] + change[FIELDS - 1 :]
    factor = jnp.exp(rate_ref[...] * jnp.tanh(heat))
    scaled = (change * factor).astype(jnp.bfloat16)
    is_heat = lax.broadcasted_iota(jnp.int32, change.shape, 0) == FIELDS - 1
    out = jnp.where(is_heat, change.astype(jnp.bfloat16), scaled)
    for r in range(rows):
        o_ref[r] = out[:, r * CHUNK : (r + 1) * CHUNK]

def surrogate_rows(x, weight_in, bias_in, weight_mid, bias_mid, weight_out, bias_out, rate):
    rows = x.shape[0]
    full = lambda shape: pl.BlockSpec(shape, lambda i: (0,) * len(shape))
    return pl.pallas_call(
        mlp_kernel,
        grid=(rows // ROW_BLOCK,),
        in_specs=[pl.BlockSpec((ROW_BLOCK, FIELDS, CHUNK), lambda i: (i, 0, 0)),
                  full(weight_in.shape), full(bias_in.shape), full(weight_mid.shape), full(bias_mid.shape),
                  full(weight_out.shape), full(bias_out.shape), full(rate.shape)],
        out_specs=pl.BlockSpec((ROW_BLOCK, FIELDS, CHUNK), lambda i: (i, 0, 0)),
        out_shape=jax.ShapeDtypeStruct((rows, FIELDS, CHUNK), jnp.bfloat16),
    )(x, weight_in, bias_in, weight_mid, bias_mid, weight_out, bias_out, rate)


def on_device(
    fields,
    zone_ids,
    diffusivity,
    heat_rate,
    weight_in,
    bias_in,
    weight_mid,
    bias_mid,
    weight_out,
    bias_out,
):
    count_here, rows_here, columns = fields.shape
    coefs = lookup(zone_ids, diffusivity)
    stacked = with_halo(jnp.concatenate([fields, coefs], 0), "space", HALO)
    fields_ext = stacked[:count_here]
    coef_pad = pad_rows(stacked[count_here:])
    first_row = lax.axis_index("space") * rows_here - HALO
    global_row = first_row + lax.broadcasted_iota(jnp.int32, (1, rows_here + 2 * HALO, 1), 1)
    inside = (global_row >= 0) & (global_row < rows_here * lax.axis_size("space"))
    state = fields_ext
    for number in range(SWEEPS):
        state = relax_step(pad_rows(state), fields_ext, coef_pad, RELAX_WEIGHTS[number])
        state = jnp.where(inside, state, jnp.float32(0.0))
    state = state[:, HALO : HALO + rows_here]

    chunks = columns // CHUNK
    outgoing = state[0].reshape(rows_here, chunks, CHUNK).transpose(1, 0, 2).astype(jnp.bfloat16)
    incoming = lax.all_to_all(outgoing, "field", 0, 0, tiled=True)
    rate = jnp.concatenate([heat_rate, jnp.zeros((FIELDS - heat_rate.shape[0],), jnp.float32)])
    delta = surrogate_rows(
        incoming.transpose(1, 0, 2),
        weight_in,
        bias_in[None],
        weight_mid,
        bias_mid[None],
        weight_out,
        bias_out[None],
        rate[:, None],
    )
    returned = lax.all_to_all(delta.transpose(1, 0, 2), "field", 0, 0, tiled=True)
    returned = returned.transpose(1, 0, 2).reshape(1, rows_here, columns)
    return state + returned.astype(jnp.float32)


def solution(mesh):
    return jax.shard_map(
        on_device,
        mesh=mesh,
        in_specs=(
            P("field", "space", None),
            P("space", None),
            P("field", None),
            P(),
            P(),
            P(),
            P(),
            P(),
            P(),
            P(),
        ),
        out_specs=P("field", "space", None),
        check_vma=False,
    )
```

```python
import jax
import jax.numpy as jnp
from jax import lax
from jax.experimental import pallas as pl
from jax.experimental.pallas import tpu as pltpu
from jax.sharding import PartitionSpec as P

FIELDS = 16
SWEEPS = 3
HALO = SWEEPS
CHUNK = 384
ROW_BLOCK = 8
NT = (((1,), (1,)), ((), ()))

RELAX_WEIGHTS = (0.8, 1.25, 0.95)


def pad_rows(array):
    return jnp.pad(array, ((0, 0), (1, 1), (0, 0)))


def relax_step(padded, source, coef_pad, weight):
    middle = padded[:, 1:-1]
    coef_mid = coef_pad[:, 1:-1]
    face_north = 0.5 * (coef_mid + coef_pad[:, 2:])
    face_south = 0.5 * (coef_mid + coef_pad[:, :-2])
    face_east = 0.5 * (coef_mid + jnp.roll(coef_mid, -1, 2))
    face_west = 0.5 * (coef_mid + jnp.roll(coef_mid, 1, 2))
    diagonal = 1.0 + face_north + face_south + face_east + face_west
    image = diagonal * middle - face_north * padded[:, 2:] - face_south * padded[:, :-2]
    image = image - face_east * jnp.roll(middle, -1, 2) - face_west * jnp.roll(middle, 1, 2)
    return middle + weight * (source - image) / diagonal


def lookup_kernel(table_ref, zone_ref, o_ref):
    zone = zone_ref[...]
    level = [table_ref[0, number] for number in range(table_ref.shape[1])]
    bit = 1
    while len(level) > 1:
        pick = (zone & bit) != 0
        level = [jnp.where(pick, level[k + 1], level[k]) for k in range(0, len(level), 2)]
        bit *= 2
    o_ref[0] = level[0]


def lookup(zone_ids, diffusivity):
    return pl.pallas_call(
        lookup_kernel,
        in_specs=[
            pl.BlockSpec(memory_space=pltpu.SMEM),
            pl.BlockSpec(memory_space=pltpu.VMEM),
        ],
        out_specs=pl.BlockSpec(memory_space=pltpu.VMEM),
        out_shape=jax.ShapeDtypeStruct((1,) + zone_ids.shape, jnp.float32),
    )(diffusivity, zone_ids)


def with_halo(block, axis, width):
    count = lax.axis_size(axis)
    head = block[:, :width]
    tail = block[:, -width:]
    from_above = lax.ppermute(tail, axis, [(i, i + 1) for i in range(count - 1)])
    from_below = lax.ppermute(head, axis, [(i + 1, i) for i in range(count - 1)])
    return jnp.concatenate([from_above, block, from_below], axis=1)


def mlp_kernel(x_ref, w_in_ref, b_in_ref, w_mid_ref, b_mid_ref, w_out_ref, b_out_ref, rate_ref, o_ref):
    rows = x_ref.shape[0]
    cells = jnp.concatenate([x_ref[r].astype(jnp.float32).T for r in range(rows)], axis=0)
    inputs = cells.astype(jnp.bfloat16)
    hidden = jax.nn.silu(lax.dot_general(inputs, w_in_ref[...], NT, preferred_element_type=jnp.float32) + b_in_ref[...])
    hidden = hidden.astype(jnp.bfloat16)
    hidden = jax.nn.silu(lax.dot_general(hidden, w_mid_ref[...], NT, preferred_element_type=jnp.float32) + b_mid_ref[...])
    hidden = hidden.astype(jnp.bfloat16)
    change = lax.dot_general(hidden, w_out_ref[...], NT, preferred_element_type=jnp.float32) + b_out_ref[...]
    change = change.astype(jnp.bfloat16).astype(jnp.float32).T
    x = cells.T
    heat = x[FIELDS - 1 :] + change[FIELDS - 1 :]
    factor = jnp.exp(rate_ref[...] * jnp.tanh(heat))
    scaled = (change * factor).astype(jnp.bfloat16)
    is_heat = lax.broadcasted_iota(jnp.int32, change.shape, 0) == FIELDS - 1
    out = jnp.where(is_heat, change.astype(jnp.bfloat16), scaled)
    for r in range(rows):
        o_ref[r] = out[:, r * CHUNK : (r + 1) * CHUNK]

def surrogate_rows(x, weight_in, bias_in, weight_mid, bias_mid, weight_out, bias_out, rate):
    rows = x.shape[0]
    full = lambda shape: pl.BlockSpec(shape, lambda i: (0,) * len(shape))
    return pl.pallas_call(
        mlp_kernel,
        grid=(rows // ROW_BLOCK,),
        in_specs=[pl.BlockSpec((ROW_BLOCK, FIELDS, CHUNK), lambda i: (i, 0, 0)),
                  full(weight_in.shape), full(bias_in.shape), full(weight_mid.shape), full(bias_mid.shape),
                  full(weight_out.shape), full(bias_out.shape), full(rate.shape)],
        out_specs=pl.BlockSpec((ROW_BLOCK, FIELDS, CHUNK), lambda i: (i, 0, 0)),
        out_shape=jax.ShapeDtypeStruct((rows, FIELDS, CHUNK), jnp.bfloat16),
    )(x, weight_in, bias_in, weight_mid, bias_mid, weight_out, bias_out, rate)


def on_device(
    fields,
    zone_ids,
    diffusivity,
    heat_rate,
    weight_in,
    bias_in,
    weight_mid,
    bias_mid,
    weight_out,
    bias_out,
):
    count_here, rows_here, columns = fields.shape
    count = lax.axis_size("space")
    where = lax.axis_index("space")
    raw = jnp.concatenate([fields, zone_ids.astype(jnp.float32)[None]], 0)
    from_above = lax.ppermute(raw[:, -HALO:], "space", [(i, i + 1) for i in range(count - 1)])
    from_below = lax.ppermute(raw[:, :HALO], "space", [(i + 1, i) for i in range(count - 1)])
    coefs = lookup(zone_ids, diffusivity)
    halo_coefs = lookup(jnp.concatenate([from_above[1], from_below[1]], 0).astype(jnp.int32), diffusivity)[0]
    coef_above = jnp.where(where > 0, halo_coefs[:HALO], jnp.float32(0.0))
    coef_below = jnp.where(where < count - 1, halo_coefs[HALO:], jnp.float32(0.0))
    stacked = jnp.concatenate(
        [
            jnp.stack([from_above[0], coef_above]),
            jnp.concatenate([fields, coefs], 0),
            jnp.stack([from_below[0], coef_below]),
        ],
        axis=1,
    )
    fields_ext = stacked[:count_here]
    coef_pad = pad_rows(stacked[count_here:])
    first_row = lax.axis_index("space") * rows_here - HALO
    global_row = first_row + lax.broadcasted_iota(jnp.int32, (1, rows_here + 2 * HALO, 1), 1)
    inside = (global_row >= 0) & (global_row < rows_here * lax.axis_size("space"))
    state = fields_ext
    for number in range(SWEEPS):
        state = relax_step(pad_rows(state), fields_ext, coef_pad, RELAX_WEIGHTS[number])
        state = jnp.where(inside, state, jnp.float32(0.0))
    state = state[:, HALO : HALO + rows_here]

    chunks = columns // CHUNK
    outgoing = state[0].reshape(rows_here, chunks, CHUNK).transpose(1, 0, 2).astype(jnp.bfloat16)
    incoming = lax.all_to_all(outgoing, "field", 0, 0, tiled=True)
    rate = jnp.concatenate([heat_rate, jnp.zeros((FIELDS - heat_rate.shape[0],), jnp.float32)])
    delta = surrogate_rows(
        incoming.transpose(1, 0, 2),
        weight_in,
        bias_in[None],
        weight_mid,
        bias_mid[None],
        weight_out,
        bias_out[None],
        rate[:, None],
    )
    returned = lax.all_to_all(delta.transpose(1, 0, 2), "field", 0, 0, tiled=True)
    returned = returned.transpose(1, 0, 2).reshape(1, rows_here, columns)
    return state + returned.astype(jnp.float32)


def solution(mesh):
    return jax.shard_map(
        on_device,
        mesh=mesh,
        in_specs=(
            P("field", "space", None),
            P("space", None),
            P("field", None),
            P(),
            P(),
            P(),
            P(),
            P(),
            P(),
            P(),
        ),
        out_specs=P("field", "space", None),
        check_vma=False,
    )
```

```python
import jax
import jax.numpy as jnp
from jax import lax
from jax.experimental import pallas as pl
from jax.experimental.pallas import tpu as pltpu
from jax.sharding import PartitionSpec as P

FIELDS = 16
SWEEPS = 3
HALO = SWEEPS
CHUNK = 384
ROW_BLOCK = 8
NT = (((1,), (1,)), ((), ()))

RELAX_WEIGHTS = (0.8, 1.25, 0.95)


def pad_rows(array):
    return jnp.pad(array, ((0, 0), (1, 1), (0, 0)))


def relax_step(padded, source, coef_pad, weight):
    middle = padded[:, 1:-1]
    coef_mid = coef_pad[:, 1:-1]
    face_north = 0.5 * (coef_mid + coef_pad[:, 2:])
    face_south = 0.5 * (coef_mid + coef_pad[:, :-2])
    face_east = 0.5 * (coef_mid + jnp.roll(coef_mid, -1, 2))
    face_west = 0.5 * (coef_mid + jnp.roll(coef_mid, 1, 2))
    diagonal = 1.0 + face_north + face_south + face_east + face_west
    image = diagonal * middle - face_north * padded[:, 2:] - face_south * padded[:, :-2]
    image = image - face_east * jnp.roll(middle, -1, 2) - face_west * jnp.roll(middle, 1, 2)
    return middle + weight * (source - image) / diagonal


def lookup_kernel(table_ref, zone_ref, o_ref):
    zone = zone_ref[...]
    level = [table_ref[0, number] for number in range(table_ref.shape[1])]
    bit = 1
    while len(level) > 1:
        pick = (zone & bit) != 0
        level = [jnp.where(pick, level[k + 1], level[k]) for k in range(0, len(level), 2)]
        bit *= 2
    o_ref[0] = level[0]


def lookup(zone_ids, diffusivity):
    return pl.pallas_call(
        lookup_kernel,
        in_specs=[
            pl.BlockSpec(memory_space=pltpu.SMEM),
            pl.BlockSpec(memory_space=pltpu.VMEM),
        ],
        out_specs=pl.BlockSpec(memory_space=pltpu.VMEM),
        out_shape=jax.ShapeDtypeStruct((1,) + zone_ids.shape, jnp.float32),
    )(diffusivity, zone_ids)


def with_halo(block, axis, width):
    count = lax.axis_size(axis)
    where = lax.axis_index(axis)
    head = block[:, :width]
    tail = block[:, -width:]
    from_above = lax.ppermute(tail, axis, [(i, (i + 1) % count) for i in range(count)])
    from_below = lax.ppermute(head, axis, [((i + 1) % count, i) for i in range(count)])
    from_above = jnp.where(where > 0, from_above, jnp.zeros_like(from_above))
    from_below = jnp.where(where < count - 1, from_below, jnp.zeros_like(from_below))
    return jnp.concatenate([from_above, block, from_below], axis=1)


def mlp_kernel(x_ref, w_in_ref, b_in_ref, w_mid_ref, b_mid_ref, w_out_ref, b_out_ref, rate_ref, o_ref):
    rows = x_ref.shape[0]
    cells = jnp.concatenate([x_ref[r].astype(jnp.float32).T for r in range(rows)], axis=0)
    inputs = cells.astype(jnp.bfloat16)
    hidden = jax.nn.silu(lax.dot_general(inputs, w_in_ref[...], NT, preferred_element_type=jnp.float32) + b_in_ref[...])
    hidden = hidden.astype(jnp.bfloat16)
    hidden = jax.nn.silu(lax.dot_general(hidden, w_mid_ref[...], NT, preferred_element_type=jnp.float32) + b_mid_ref[...])
    hidden = hidden.astype(jnp.bfloat16)
    change = lax.dot_general(hidden, w_out_ref[...], NT, preferred_element_type=jnp.float32) + b_out_ref[...]
    change = change.astype(jnp.bfloat16).astype(jnp.float32).T
    x = cells.T
    heat = x[FIELDS - 1 :] + change[FIELDS - 1 :]
    factor = jnp.exp(rate_ref[...] * jnp.tanh(heat))
    scaled = (change * factor).astype(jnp.bfloat16)
    is_heat = lax.broadcasted_iota(jnp.int32, change.shape, 0) == FIELDS - 1
    out = jnp.where(is_heat, change.astype(jnp.bfloat16), scaled)
    for r in range(rows):
        o_ref[r] = out[:, r * CHUNK : (r + 1) * CHUNK]

def surrogate_rows(x, weight_in, bias_in, weight_mid, bias_mid, weight_out, bias_out, rate):
    rows = x.shape[0]
    full = lambda shape: pl.BlockSpec(shape, lambda i: (0,) * len(shape))
    return pl.pallas_call(
        mlp_kernel,
        grid=(rows // ROW_BLOCK,),
        in_specs=[pl.BlockSpec((ROW_BLOCK, FIELDS, CHUNK), lambda i: (i, 0, 0)),
                  full(weight_in.shape), full(bias_in.shape), full(weight_mid.shape), full(bias_mid.shape),
                  full(weight_out.shape), full(bias_out.shape), full(rate.shape)],
        out_specs=pl.BlockSpec((ROW_BLOCK, FIELDS, CHUNK), lambda i: (i, 0, 0)),
        out_shape=jax.ShapeDtypeStruct((rows, FIELDS, CHUNK), jnp.bfloat16),
    )(x, weight_in, bias_in, weight_mid, bias_mid, weight_out, bias_out, rate)


def on_device(
    fields,
    zone_ids,
    diffusivity,
    heat_rate,
    weight_in,
    bias_in,
    weight_mid,
    bias_mid,
    weight_out,
    bias_out,
):
    count_here, rows_here, columns = fields.shape
    coefs = lookup(zone_ids, diffusivity)
    stacked = with_halo(jnp.concatenate([fields, coefs], 0), "space", HALO)
    fields_ext = stacked[:count_here]
    coef_pad = pad_rows(stacked[count_here:])
    first_row = lax.axis_index("space") * rows_here - HALO
    global_row = first_row + lax.broadcasted_iota(jnp.int32, (1, rows_here + 2 * HALO, 1), 1)
    inside = (global_row >= 0) & (global_row < rows_here * lax.axis_size("space"))
    state = fields_ext
    for number in range(SWEEPS):
        state = relax_step(pad_rows(state), fields_ext, coef_pad, RELAX_WEIGHTS[number])
        state = jnp.where(inside, state, jnp.float32(0.0))
    state = state[:, HALO : HALO + rows_here]

    chunks = columns // CHUNK
    outgoing = state[0].reshape(rows_here, chunks, CHUNK).transpose(1, 0, 2).astype(jnp.bfloat16)
    incoming = lax.all_to_all(outgoing, "field", 0, 0, tiled=True)
    rate = jnp.concatenate([heat_rate, jnp.zeros((FIELDS - heat_rate.shape[0],), jnp.float32)])
    delta = surrogate_rows(
        incoming.transpose(1, 0, 2),
        weight_in,
        bias_in[None],
        weight_mid,
        bias_mid[None],
        weight_out,
        bias_out[None],
        rate[:, None],
    )
    returned = lax.all_to_all(delta.transpose(1, 0, 2), "field", 0, 0, tiled=True)
    returned = returned.transpose(1, 0, 2).reshape(1, rows_here, columns)
    return state + returned.astype(jnp.float32)


def solution(mesh):
    return jax.shard_map(
        on_device,
        mesh=mesh,
        in_specs=(
            P("field", "space", None),
            P("space", None),
            P("field", None),
            P(),
            P(),
            P(),
            P(),
            P(),
            P(),
            P(),
        ),
        out_specs=P("field", "space", None),
        check_vma=False,
    )
```

```python
import jax
import jax.numpy as jnp
from jax import lax
from jax.experimental import pallas as pl
from jax.experimental.pallas import tpu as pltpu
from jax.sharding import PartitionSpec as P

FIELDS = 16
SWEEPS = 3
HALO = SWEEPS
CHUNK = 384
ROW_BLOCK = 32
NT = (((1,), (1,)), ((), ()))

RELAX_WEIGHTS = (0.8, 1.25, 0.95)


def pad_rows(array):
    return jnp.pad(array, ((0, 0), (1, 1), (0, 0)))


def relax_step(padded, source, coef_pad, weight):
    middle = padded[:, 1:-1]
    coef_mid = coef_pad[:, 1:-1]
    face_north = 0.5 * (coef_mid + coef_pad[:, 2:])
    face_south = 0.5 * (coef_mid + coef_pad[:, :-2])
    face_east = 0.5 * (coef_mid + jnp.roll(coef_mid, -1, 2))
    face_west = 0.5 * (coef_mid + jnp.roll(coef_mid, 1, 2))
    diagonal = 1.0 + face_north + face_south + face_east + face_west
    image = diagonal * middle - face_north * padded[:, 2:] - face_south * padded[:, :-2]
    image = image - face_east * jnp.roll(middle, -1, 2) - face_west * jnp.roll(middle, 1, 2)
    return middle + weight * (source - image) / diagonal


def lookup_kernel(table_ref, zone_ref, o_ref):
    zone = zone_ref[...]
    level = [table_ref[0, number] for number in range(table_ref.shape[1])]
    bit = 1
    while len(level) > 1:
        pick = (zone & bit) != 0
        level = [jnp.where(pick, level[k + 1], level[k]) for k in range(0, len(level), 2)]
        bit *= 2
    o_ref[0] = level[0]


def lookup(zone_ids, diffusivity):
    return pl.pallas_call(
        lookup_kernel,
        in_specs=[
            pl.BlockSpec(memory_space=pltpu.SMEM),
            pl.BlockSpec(memory_space=pltpu.VMEM),
        ],
        out_specs=pl.BlockSpec(memory_space=pltpu.VMEM),
        out_shape=jax.ShapeDtypeStruct((1,) + zone_ids.shape, jnp.float32),
    )(diffusivity, zone_ids)


def with_halo(block, axis, width):
    count = lax.axis_size(axis)
    head = block[:, :width]
    tail = block[:, -width:]
    from_above = lax.ppermute(tail, axis, [(i, i + 1) for i in range(count - 1)])
    from_below = lax.ppermute(head, axis, [(i + 1, i) for i in range(count - 1)])
    return jnp.concatenate([from_above, block, from_below], axis=1)


def mlp_kernel(x_ref, w_in_ref, b_in_ref, w_mid_ref, b_mid_ref, w_out_ref, b_out_ref, rate_ref, o_ref):
    rows = x_ref.shape[1]
    block = x_ref[...].astype(jnp.float32)
    cells = jnp.concatenate([block[:, r, :].T for r in range(rows)], axis=0)
    inputs = cells.astype(jnp.bfloat16)
    hidden = jax.nn.silu(lax.dot_general(inputs, w_in_ref[...], NT, preferred_element_type=jnp.float32) + b_in_ref[...])
    hidden = hidden.astype(jnp.bfloat16)
    hidden = jax.nn.silu(lax.dot_general(hidden, w_mid_ref[...], NT, preferred_element_type=jnp.float32) + b_mid_ref[...])
    hidden = hidden.astype(jnp.bfloat16)
    change = lax.dot_general(hidden, w_out_ref[...], NT, preferred_element_type=jnp.float32) + b_out_ref[...]
    change = change.astype(jnp.bfloat16).astype(jnp.float32).T
    x = cells.T
    heat = x[FIELDS - 1 :] + change[FIELDS - 1 :]
    factor = jnp.exp(rate_ref[...] * jnp.tanh(heat))
    scaled = (change * factor).astype(jnp.bfloat16)
    is_heat = lax.broadcasted_iota(jnp.int32, change.shape, 0) == FIELDS - 1
    out = jnp.where(is_heat, change.astype(jnp.bfloat16), scaled).astype(jnp.float32)
    rows_out = [out[:, r * CHUNK : (r + 1) * CHUNK] for r in range(rows)]
    o_ref[...] = jnp.stack(rows_out, axis=1).astype(jnp.bfloat16)


def surrogate_rows(x, weight_in, bias_in, weight_mid, bias_mid, weight_out, bias_out, rate):
    rows = x.shape[1]
    full = lambda shape: pl.BlockSpec(shape, lambda i: (0,) * len(shape))
    return pl.pallas_call(
        mlp_kernel,
        grid=(rows // ROW_BLOCK,),
        in_specs=[
            pl.BlockSpec((FIELDS, ROW_BLOCK, CHUNK), lambda i: (0, i, 0)),
            full(weight_in.shape),
            full(bias_in.shape),
            full(weight_mid.shape),
            full(bias_mid.shape),
            full(weight_out.shape),
            full(bias_out.shape),
            full(rate.shape),
        ],
        out_specs=pl.BlockSpec((FIELDS, ROW_BLOCK, CHUNK), lambda i: (0, i, 0)),
        out_shape=jax.ShapeDtypeStruct(x.shape, jnp.bfloat16),
    )(x, weight_in, bias_in, weight_mid, bias_mid, weight_out, bias_out, rate)


def on_device(
    fields,
    zone_ids,
    diffusivity,
    heat_rate,
    weight_in,
    bias_in,
    weight_mid,
    bias_mid,
    weight_out,
    bias_out,
):
    count_here, rows_here, columns = fields.shape
    coefs = lookup(zone_ids, diffusivity)
    stacked = with_halo(jnp.concatenate([fields, coefs], 0), "space", HALO)
    fields_ext = stacked[:count_here]
    coef_pad = pad_rows(stacked[count_here:])
    first_row = lax.axis_index("space") * rows_here - HALO
    global_row = first_row + lax.broadcasted_iota(jnp.int32, (1, rows_here + 2 * HALO, 1), 1)
    inside = (global_row >= 0) & (global_row < rows_here * lax.axis_size("space"))
    state = fields_ext
    for number in range(SWEEPS):
        state = relax_step(pad_rows(state), fields_ext, coef_pad, RELAX_WEIGHTS[number])
        state = jnp.where(inside, state, jnp.float32(0.0))
    state = state[:, HALO : HALO + rows_here]

    chunks = columns // CHUNK
    outgoing = state[0].reshape(rows_here, chunks, CHUNK).transpose(1, 0, 2).astype(jnp.bfloat16)
    incoming = lax.all_to_all(outgoing, "field", 0, 0, tiled=True)
    rate = jnp.concatenate([heat_rate, jnp.zeros((FIELDS - heat_rate.shape[0],), jnp.float32)])
    delta = surrogate_rows(
        incoming,
        weight_in,
        bias_in[None],
        weight_mid,
        bias_mid[None],
        weight_out,
        bias_out[None],
        rate[:, None],
    )
    returned = lax.all_to_all(delta, "field", 0, 0, tiled=True)
    returned = returned.transpose(1, 0, 2).reshape(1, rows_here, columns)
    return state + returned.astype(jnp.float32)


def solution(mesh):
    return jax.shard_map(
        on_device,
        mesh=mesh,
        in_specs=(
            P("field", "space", None),
            P("space", None),
            P("field", None),
            P(),
            P(),
            P(),
            P(),
            P(),
            P(),
            P(),
        ),
        out_specs=P("field", "space", None),
        check_vma=False,
    )
```

```python
import jax
import jax.numpy as jnp
from jax import lax
from jax.experimental import pallas as pl
from jax.experimental.pallas import tpu as pltpu
from jax.sharding import PartitionSpec as P

FIELDS = 16
SWEEPS = 3
HALO = SWEEPS
CHUNK = 384
ROW_BLOCK = 16
NT = (((1,), (1,)), ((), ()))

RELAX_WEIGHTS = (0.8, 1.25, 0.95)


def pad_rows(array):
    return jnp.pad(array, ((0, 0), (1, 1), (0, 0)))


def relax_step(padded, source, coef_pad, weight):
    middle = padded[:, 1:-1]
    coef_mid = coef_pad[:, 1:-1]
    face_north = 0.5 * (coef_mid + coef_pad[:, 2:])
    face_south = 0.5 * (coef_mid + coef_pad[:, :-2])
    face_east = 0.5 * (coef_mid + jnp.roll(coef_mid, -1, 2))
    face_west = 0.5 * (coef_mid + jnp.roll(coef_mid, 1, 2))
    diagonal = 1.0 + face_north + face_south + face_east + face_west
    image = diagonal * middle - face_north * padded[:, 2:] - face_south * padded[:, :-2]
    image = image - face_east * jnp.roll(middle, -1, 2) - face_west * jnp.roll(middle, 1, 2)
    return middle + weight * (source - image) / diagonal


def lookup_kernel(table_ref, zone_ref, o_ref):
    zone = zone_ref[...]
    level = [table_ref[0, number] for number in range(table_ref.shape[1])]
    bit = 1
    while len(level) > 1:
        pick = (zone & bit) != 0
        level = [jnp.where(pick, level[k + 1], level[k]) for k in range(0, len(level), 2)]
        bit *= 2
    o_ref[0] = level[0]


def lookup(zone_ids, diffusivity):
    return pl.pallas_call(
        lookup_kernel,
        in_specs=[
            pl.BlockSpec(memory_space=pltpu.SMEM),
            pl.BlockSpec(memory_space=pltpu.VMEM),
        ],
        out_specs=pl.BlockSpec(memory_space=pltpu.VMEM),
        out_shape=jax.ShapeDtypeStruct((1,) + zone_ids.shape, jnp.float32),
    )(diffusivity, zone_ids)


def with_halo(block, axis, width):
    count = lax.axis_size(axis)
    head = block[:, :width]
    tail = block[:, -width:]
    from_above = lax.ppermute(tail, axis, [(i, i + 1) for i in range(count - 1)])
    from_below = lax.ppermute(head, axis, [(i + 1, i) for i in range(count - 1)])
    return jnp.concatenate([from_above, block, from_below], axis=1)


def mlp_kernel(x_ref, w_in_ref, b_in_ref, w_mid_ref, b_mid_ref, w_out_ref, b_out_ref, rate_ref, o_ref):
    rows = x_ref.shape[1]
    block = x_ref[...].astype(jnp.float32)
    cells = jnp.concatenate([block[:, r, :].T for r in range(rows)], axis=0)
    inputs = cells.astype(jnp.bfloat16)
    hidden = jax.nn.silu(lax.dot_general(inputs, w_in_ref[...], NT, preferred_element_type=jnp.float32) + b_in_ref[...])
    hidden = hidden.astype(jnp.bfloat16)
    hidden = jax.nn.silu(lax.dot_general(hidden, w_mid_ref[...], NT, preferred_element_type=jnp.float32) + b_mid_ref[...])
    hidden = hidden.astype(jnp.bfloat16)
    change = lax.dot_general(hidden, w_out_ref[...], NT, preferred_element_type=jnp.float32) + b_out_ref[...]
    change = change.astype(jnp.bfloat16).astype(jnp.float32).T
    x = cells.T
    heat = x[FIELDS - 1 :] + change[FIELDS - 1 :]
    factor = jnp.exp(rate_ref[...] * jnp.tanh(heat))
    scaled = (change * factor).astype(jnp.bfloat16)
    is_heat = lax.broadcasted_iota(jnp.int32, change.shape, 0) == FIELDS - 1
    out = jnp.where(is_heat, change.astype(jnp.bfloat16), scaled).astype(jnp.float32)
    rows_out = [out[:, r * CHUNK : (r + 1) * CHUNK] for r in range(rows)]
    o_ref[...] = jnp.stack(rows_out, axis=1).astype(jnp.bfloat16)


def surrogate_rows(x, weight_in, bias_in, weight_mid, bias_mid, weight_out, bias_out, rate):
    rows = x.shape[1]
    full = lambda shape: pl.BlockSpec(shape, lambda i: (0,) * len(shape))
    return pl.pallas_call(
        mlp_kernel,
        grid=(rows // ROW_BLOCK,),
        in_specs=[
            pl.BlockSpec((FIELDS, ROW_BLOCK, CHUNK), lambda i: (0, i, 0)),
            full(weight_in.shape),
            full(bias_in.shape),
            full(weight_mid.shape),
            full(bias_mid.shape),
            full(weight_out.shape),
            full(bias_out.shape),
            full(rate.shape),
        ],
        out_specs=pl.BlockSpec((FIELDS, ROW_BLOCK, CHUNK), lambda i: (0, i, 0)),
        out_shape=jax.ShapeDtypeStruct(x.shape, jnp.bfloat16),
    )(x, weight_in, bias_in, weight_mid, bias_mid, weight_out, bias_out, rate)


def on_device(
    fields,
    zone_ids,
    diffusivity,
    heat_rate,
    weight_in,
    bias_in,
    weight_mid,
    bias_mid,
    weight_out,
    bias_out,
):
    count_here, rows_here, columns = fields.shape
    coefs = lookup(zone_ids, diffusivity)
    stacked = with_halo(jnp.concatenate([fields, coefs], 0), "space", HALO)
    fields_ext = stacked[:count_here]
    coef_pad = pad_rows(stacked[count_here:])
    first_row = lax.axis_index("space") * rows_here - HALO
    global_row = first_row + lax.broadcasted_iota(jnp.int32, (1, rows_here + 2 * HALO, 1), 1)
    inside = (global_row >= 0) & (global_row < rows_here * lax.axis_size("space"))
    state = fields_ext
    for number in range(SWEEPS):
        state = relax_step(pad_rows(state), fields_ext, coef_pad, RELAX_WEIGHTS[number])
        state = jnp.where(inside, state, jnp.float32(0.0))
    state = state[:, HALO : HALO + rows_here]

    chunks = columns // CHUNK
    outgoing = state[0].reshape(rows_here, chunks, CHUNK).transpose(1, 0, 2).astype(jnp.bfloat16)
    incoming = lax.all_to_all(outgoing, "field", 0, 0, tiled=True)
    rate = jnp.concatenate([heat_rate, jnp.zeros((FIELDS - heat_rate.shape[0],), jnp.float32)])
    delta = surrogate_rows(
        incoming,
        weight_in,
        bias_in[None],
        weight_mid,
        bias_mid[None],
        weight_out,
        bias_out[None],
        rate[:, None],
    )
    returned = lax.all_to_all(delta, "field", 0, 0, tiled=True)
    returned = returned.transpose(1, 0, 2).reshape(1, rows_here, columns)
    return state + returned.astype(jnp.float32)


def solution(mesh):
    return jax.shard_map(
        on_device,
        mesh=mesh,
        in_specs=(
            P("field", "space", None),
            P("space", None),
            P("field", None),
            P(),
            P(),
            P(),
            P(),
            P(),
            P(),
            P(),
        ),
        out_specs=P("field", "space", None),
        check_vma=False,
    )
```

```python
import jax
import jax.numpy as jnp
from jax import lax
from jax.experimental import pallas as pl
from jax.experimental.pallas import tpu as pltpu
from jax.sharding import PartitionSpec as P

FIELDS = 16
SWEEPS = 3
HALO = SWEEPS
CHUNK = 384
ROW_BLOCK = 8
NT = (((1,), (1,)), ((), ()))

RELAX_WEIGHTS = (0.8, 1.25, 0.95)


def pad_rows(array):
    return jnp.pad(array, ((0, 0), (1, 1), (0, 0)))


def relax_step(padded, source, coef_pad, weight):
    middle = padded[:, 1:-1]
    coef_mid = coef_pad[:, 1:-1]
    face_north = 0.5 * (coef_mid + coef_pad[:, 2:])
    face_south = 0.5 * (coef_mid + coef_pad[:, :-2])
    face_east = 0.5 * (coef_mid + jnp.roll(coef_mid, -1, 2))
    face_west = 0.5 * (coef_mid + jnp.roll(coef_mid, 1, 2))
    diagonal = 1.0 + face_north + face_south + face_east + face_west
    image = diagonal * middle - face_north * padded[:, 2:] - face_south * padded[:, :-2]
    image = image - face_east * jnp.roll(middle, -1, 2) - face_west * jnp.roll(middle, 1, 2)
    return middle + weight * (source - image) / diagonal


def lookup_kernel(table_ref, zone_ref, fields_ref, o_ref, head_ref, tail_ref):
    zone = zone_ref[...]
    level = [table_ref[0, number] for number in range(table_ref.shape[1])]
    bit = 1
    while len(level) > 1:
        pick = (zone & bit) != 0
        level = [jnp.where(pick, level[k + 1], level[k]) for k in range(0, len(level), 2)]
        bit *= 2
    coef = level[0]
    o_ref[0] = coef
    width = head_ref.shape[1]
    here = fields_ref[0]
    head_ref[0] = here[:width]
    head_ref[1] = coef[:width]
    tail_ref[0] = here[-width:]
    tail_ref[1] = coef[-width:]


def lookup(zone_ids, diffusivity, fields, width):
    rows, cols = zone_ids.shape
    return pl.pallas_call(
        lookup_kernel,
        in_specs=[
            pl.BlockSpec(memory_space=pltpu.SMEM),
            pl.BlockSpec(memory_space=pltpu.VMEM),
            pl.BlockSpec(memory_space=pltpu.VMEM),
        ],
        out_specs=[pl.BlockSpec(memory_space=pltpu.VMEM)] * 3,
        out_shape=[
            jax.ShapeDtypeStruct((1, rows, cols), jnp.float32),
            jax.ShapeDtypeStruct((2, width, cols), jnp.float32),
            jax.ShapeDtypeStruct((2, width, cols), jnp.float32),
        ],
    )(diffusivity, zone_ids, fields)


def with_halo(block, head, tail, axis):
    count = lax.axis_size(axis)
    from_above = lax.ppermute(tail, axis, [(i, i + 1) for i in range(count - 1)])
    from_below = lax.ppermute(head, axis, [(i + 1, i) for i in range(count - 1)])
    return jnp.concatenate([from_above, block, from_below], axis=1)


def mlp_kernel(x_ref, w_in_ref, b_in_ref, w_mid_ref, b_mid_ref, w_out_ref, b_out_ref, rate_ref, o_ref):
    rows = x_ref.shape[0]
    cells = jnp.concatenate([x_ref[r].astype(jnp.float32).T for r in range(rows)], axis=0)
    inputs = cells.astype(jnp.bfloat16)
    hidden = jax.nn.silu(lax.dot_general(inputs, w_in_ref[...], NT, preferred_element_type=jnp.float32) + b_in_ref[...])
    hidden = hidden.astype(jnp.bfloat16)
    hidden = jax.nn.silu(lax.dot_general(hidden, w_mid_ref[...], NT, preferred_element_type=jnp.float32) + b_mid_ref[...])
    hidden = hidden.astype(jnp.bfloat16)
    change = lax.dot_general(hidden, w_out_ref[...], NT, preferred_element_type=jnp.float32) + b_out_ref[...]
    change = change.astype(jnp.bfloat16).astype(jnp.float32).T
    x = cells.T
    heat = x[FIELDS - 1 :] + change[FIELDS - 1 :]
    factor = jnp.exp(rate_ref[...] * jnp.tanh(heat))
    scaled = (change * factor).astype(jnp.bfloat16)
    is_heat = lax.broadcasted_iota(jnp.int32, change.shape, 0) == FIELDS - 1
    out = jnp.where(is_heat, change.astype(jnp.bfloat16), scaled)
    for r in range(rows):
        o_ref[r] = out[:, r * CHUNK : (r + 1) * CHUNK]

def surrogate_rows(x, weight_in, bias_in, weight_mid, bias_mid, weight_out, bias_out, rate):
    rows = x.shape[0]
    full = lambda shape: pl.BlockSpec(shape, lambda i: (0,) * len(shape))
    return pl.pallas_call(
        mlp_kernel,
        grid=(rows // ROW_BLOCK,),
        in_specs=[pl.BlockSpec((ROW_BLOCK, FIELDS, CHUNK), lambda i: (i, 0, 0)),
                  full(weight_in.shape), full(bias_in.shape), full(weight_mid.shape), full(bias_mid.shape),
                  full(weight_out.shape), full(bias_out.shape), full(rate.shape)],
        out_specs=pl.BlockSpec((ROW_BLOCK, FIELDS, CHUNK), lambda i: (i, 0, 0)),
        out_shape=jax.ShapeDtypeStruct((rows, FIELDS, CHUNK), jnp.bfloat16),
    )(x, weight_in, bias_in, weight_mid, bias_mid, weight_out, bias_out, rate)


def on_device(
    fields,
    zone_ids,
    diffusivity,
    heat_rate,
    weight_in,
    bias_in,
    weight_mid,
    bias_mid,
    weight_out,
    bias_out,
):
    count_here, rows_here, columns = fields.shape
    coefs, head, tail = lookup(zone_ids, diffusivity, fields, HALO)
    stacked = with_halo(jnp.concatenate([fields, coefs], 0), head, tail, "space")
    fields_ext = stacked[:count_here]
    coef_pad = pad_rows(stacked[count_here:])
    first_row = lax.axis_index("space") * rows_here - HALO
    global_row = first_row + lax.broadcasted_iota(jnp.int32, (1, rows_here + 2 * HALO, 1), 1)
    inside = (global_row >= 0) & (global_row < rows_here * lax.axis_size("space"))
    state = fields_ext
    for number in range(SWEEPS):
        state = relax_step(pad_rows(state), fields_ext, coef_pad, RELAX_WEIGHTS[number])
        state = jnp.where(inside, state, jnp.float32(0.0))
    state = state[:, HALO : HALO + rows_here]

    chunks = columns // CHUNK
    outgoing = state[0].reshape(rows_here, chunks, CHUNK).transpose(1, 0, 2).astype(jnp.bfloat16)
    incoming = lax.all_to_all(outgoing, "field", 0, 0, tiled=True)
    rate = jnp.concatenate([heat_rate, jnp.zeros((FIELDS - heat_rate.shape[0],), jnp.float32)])
    delta = surrogate_rows(
        incoming.transpose(1, 0, 2),
        weight_in,
        bias_in[None],
        weight_mid,
        bias_mid[None],
        weight_out,
        bias_out[None],
        rate[:, None],
    )
    returned = lax.all_to_all(delta.transpose(1, 0, 2), "field", 0, 0, tiled=True)
    returned = returned.transpose(1, 0, 2).reshape(1, rows_here, columns)
    return state + returned.astype(jnp.float32)


def solution(mesh):
    return jax.shard_map(
        on_device,
        mesh=mesh,
        in_specs=(
            P("field", "space", None),
            P("space", None),
            P("field", None),
            P(),
            P(),
            P(),
            P(),
            P(),
            P(),
            P(),
        ),
        out_specs=P("field", "space", None),
        check_vma=False,
    )
```

```python
import jax
import jax.numpy as jnp
from jax import lax
from jax.experimental import pallas as pl
from jax.experimental.pallas import tpu as pltpu
from jax.sharding import PartitionSpec as P

FIELDS = 16
SWEEPS = 3
HALO = SWEEPS
CHUNK = 384
ROW_BLOCK = 16
NT = (((1,), (1,)), ((), ()))

RELAX_WEIGHTS = (0.8, 1.25, 0.95)


def pad_rows(array):
    return jnp.pad(array, ((0, 0), (1, 1), (0, 0)))


def relax_step(padded, source, coef_pad, weight):
    middle = padded[:, 1:-1]
    coef_mid = coef_pad[:, 1:-1]
    face_north = 0.5 * (coef_mid + coef_pad[:, 2:])
    face_south = 0.5 * (coef_mid + coef_pad[:, :-2])
    face_east = 0.5 * (coef_mid + jnp.roll(coef_mid, -1, 2))
    face_west = 0.5 * (coef_mid + jnp.roll(coef_mid, 1, 2))
    diagonal = 1.0 + face_north + face_south + face_east + face_west
    image = diagonal * middle - face_north * padded[:, 2:] - face_south * padded[:, :-2]
    image = image - face_east * jnp.roll(middle, -1, 2) - face_west * jnp.roll(middle, 1, 2)
    return middle + weight * (source - image) / diagonal


def lookup_kernel(table_ref, zone_ref, o_ref):
    zone = zone_ref[...]
    level = [table_ref[0, number] for number in range(table_ref.shape[1])]
    bit = 1
    while len(level) > 1:
        pick = (zone & bit) != 0
        level = [jnp.where(pick, level[k + 1], level[k]) for k in range(0, len(level), 2)]
        bit *= 2
    o_ref[0] = level[0]


def lookup(zone_ids, diffusivity):
    return pl.pallas_call(
        lookup_kernel,
        in_specs=[
            pl.BlockSpec(memory_space=pltpu.SMEM),
            pl.BlockSpec(memory_space=pltpu.VMEM),
        ],
        out_specs=pl.BlockSpec(memory_space=pltpu.VMEM),
        out_shape=jax.ShapeDtypeStruct((1,) + zone_ids.shape, jnp.float32),
    )(diffusivity, zone_ids)


def with_halo(block, axis, width):
    count = lax.axis_size(axis)
    head = block[:, :width]
    tail = block[:, -width:]
    from_above = lax.ppermute(tail, axis, [(i, i + 1) for i in range(count - 1)])
    from_below = lax.ppermute(head, axis, [(i + 1, i) for i in range(count - 1)])
    return jnp.concatenate([from_above, block, from_below], axis=1)


def mlp_kernel(x_ref, w_in_ref, b_in_ref, w_mid_ref, b_mid_ref, w_out_ref, b_out_ref, rate_ref, o_ref):
    rows = x_ref.shape[0]
    cells = jnp.concatenate([x_ref[r].astype(jnp.float32).T for r in range(rows)], axis=0)
    inputs = cells.astype(jnp.bfloat16)
    hidden = jax.nn.silu(lax.dot_general(inputs, w_in_ref[...], NT, preferred_element_type=jnp.float32) + b_in_ref[...])
    hidden = hidden.astype(jnp.bfloat16)
    hidden = jax.nn.silu(lax.dot_general(hidden, w_mid_ref[...], NT, preferred_element_type=jnp.float32) + b_mid_ref[...])
    hidden = hidden.astype(jnp.bfloat16)
    change = lax.dot_general(hidden, w_out_ref[...], NT, preferred_element_type=jnp.float32) + b_out_ref[...]
    change = change.astype(jnp.bfloat16).astype(jnp.float32).T
    x = cells.T
    heat = x[FIELDS - 1 :] + change[FIELDS - 1 :]
    factor = jnp.exp(rate_ref[...] * jnp.tanh(heat))
    scaled = (change * factor).astype(jnp.bfloat16)
    is_heat = lax.broadcasted_iota(jnp.int32, change.shape, 0) == FIELDS - 1
    out = jnp.where(is_heat, change.astype(jnp.bfloat16), scaled)
    for r in range(rows):
        o_ref[r] = out[:, r * CHUNK : (r + 1) * CHUNK]

def surrogate_rows(x, weight_in, bias_in, weight_mid, bias_mid, weight_out, bias_out, rate):
    rows = x.shape[0]
    full = lambda shape: pl.BlockSpec(shape, lambda i: (0,) * len(shape))
    return pl.pallas_call(
        mlp_kernel,
        grid=(rows // ROW_BLOCK,),
        in_specs=[pl.BlockSpec((ROW_BLOCK, FIELDS, CHUNK), lambda i: (i, 0, 0)),
                  full(weight_in.shape), full(bias_in.shape), full(weight_mid.shape), full(bias_mid.shape),
                  full(weight_out.shape), full(bias_out.shape), full(rate.shape)],
        out_specs=pl.BlockSpec((ROW_BLOCK, FIELDS, CHUNK), lambda i: (i, 0, 0)),
        out_shape=jax.ShapeDtypeStruct((rows, FIELDS, CHUNK), jnp.bfloat16),
    )(x, weight_in, bias_in, weight_mid, bias_mid, weight_out, bias_out, rate)


def on_device(
    fields,
    zone_ids,
    diffusivity,
    heat_rate,
    weight_in,
    bias_in,
    weight_mid,
    bias_mid,
    weight_out,
    bias_out,
):
    count_here, rows_here, columns = fields.shape
    coefs = lookup(zone_ids, diffusivity)
    stacked = with_halo(jnp.concatenate([fields, coefs], 0), "space", HALO)
    fields_ext = stacked[:count_here]
    coef_pad = pad_rows(stacked[count_here:])
    first_row = lax.axis_index("space") * rows_here - HALO
    global_row = first_row + lax.broadcasted_iota(jnp.int32, (1, rows_here + 2 * HALO, 1), 1)
    inside = (global_row >= 0) & (global_row < rows_here * lax.axis_size("space"))
    state = fields_ext
    for number in range(SWEEPS):
        state = relax_step(pad_rows(state), fields_ext, coef_pad, RELAX_WEIGHTS[number])
        state = jnp.where(inside, state, jnp.float32(0.0))
    state = state[:, HALO : HALO + rows_here]

    chunks = columns // CHUNK
    outgoing = state[0].reshape(rows_here, chunks, CHUNK).transpose(1, 0, 2).astype(jnp.bfloat16)
    incoming = lax.all_to_all(outgoing, "field", 0, 0, tiled=True)
    rate = jnp.concatenate([heat_rate, jnp.zeros((FIELDS - heat_rate.shape[0],), jnp.float32)])
    delta = surrogate_rows(
        incoming.transpose(1, 0, 2),
        weight_in,
        bias_in[None],
        weight_mid,
        bias_mid[None],
        weight_out,
        bias_out[None],
        rate[:, None],
    )
    returned = lax.all_to_all(delta.transpose(1, 0, 2), "field", 0, 0, tiled=True)
    returned = returned.transpose(1, 0, 2).reshape(1, rows_here, columns)
    return state + returned.astype(jnp.float32)


def solution(mesh):
    return jax.shard_map(
        on_device,
        mesh=mesh,
        in_specs=(
            P("field", "space", None),
            P("space", None),
            P("field", None),
            P(),
            P(),
            P(),
            P(),
            P(),
            P(),
            P(),
        ),
        out_specs=P("field", "space", None),
        check_vma=False,
    )
```

```python
import jax
import jax.numpy as jnp
from jax import lax
from jax.experimental import pallas as pl
from jax.experimental.pallas import tpu as pltpu
from jax.sharding import PartitionSpec as P

FIELDS = 16
SWEEPS = 3
HALO = SWEEPS
CHUNK = 384
ROW_BLOCK = 32
NT = (((1,), (1,)), ((), ()))

RELAX_WEIGHTS = (0.8, 1.25, 0.95)


def pad_rows(array):
    return jnp.pad(array, ((0, 0), (1, 1), (0, 0)))


def relax_step(padded, source, coef_pad, weight):
    middle = padded[:, 1:-1]
    coef_mid = coef_pad[:, 1:-1]
    face_north = 0.5 * (coef_mid + coef_pad[:, 2:])
    face_south = 0.5 * (coef_mid + coef_pad[:, :-2])
    face_east = 0.5 * (coef_mid + jnp.roll(coef_mid, -1, 2))
    face_west = 0.5 * (coef_mid + jnp.roll(coef_mid, 1, 2))
    diagonal = 1.0 + face_north + face_south + face_east + face_west
    image = diagonal * middle - face_north * padded[:, 2:] - face_south * padded[:, :-2]
    image = image - face_east * jnp.roll(middle, -1, 2) - face_west * jnp.roll(middle, 1, 2)
    return middle + weight * (source - image) / diagonal


def lookup_kernel(table_ref, zone_ref, o_ref):
    zone = zone_ref[...]
    level = [table_ref[0, number] for number in range(table_ref.shape[1])]
    bit = 1
    while len(level) > 1:
        pick = (zone & bit) != 0
        level = [jnp.where(pick, level[k + 1], level[k]) for k in range(0, len(level), 2)]
        bit *= 2
    o_ref[0] = level[0]


def lookup(zone_ids, diffusivity):
    return pl.pallas_call(
        lookup_kernel,
        in_specs=[
            pl.BlockSpec(memory_space=pltpu.SMEM),
            pl.BlockSpec(memory_space=pltpu.VMEM),
        ],
        out_specs=pl.BlockSpec(memory_space=pltpu.VMEM),
        out_shape=jax.ShapeDtypeStruct((1,) + zone_ids.shape, jnp.float32),
    )(diffusivity, zone_ids)


def with_halo(block, axis, width):
    count = lax.axis_size(axis)
    head = block[:, :width]
    tail = block[:, -width:]
    from_above = lax.ppermute(tail, axis, [(i, i + 1) for i in range(count - 1)])
    from_below = lax.ppermute(head, axis, [(i + 1, i) for i in range(count - 1)])
    return jnp.concatenate([from_above, block, from_below], axis=1)


def mlp_kernel(x_ref, w_in_ref, b_in_ref, w_mid_ref, b_mid_ref, w_out_ref, b_out_ref, rate_ref, o_ref):
    rows = x_ref.shape[0]
    cells = jnp.concatenate([x_ref[r].astype(jnp.float32).T for r in range(rows)], axis=0)
    inputs = cells.astype(jnp.bfloat16)
    hidden = jax.nn.silu(lax.dot_general(inputs, w_in_ref[...], NT, preferred_element_type=jnp.float32) + b_in_ref[...])
    hidden = hidden.astype(jnp.bfloat16)
    hidden = jax.nn.silu(lax.dot_general(hidden, w_mid_ref[...], NT, preferred_element_type=jnp.float32) + b_mid_ref[...])
    hidden = hidden.astype(jnp.bfloat16)
    change = lax.dot_general(hidden, w_out_ref[...], NT, preferred_element_type=jnp.float32) + b_out_ref[...]
    change = change.astype(jnp.bfloat16).astype(jnp.float32).T
    x = cells.T
    heat = x[FIELDS - 1 :] + change[FIELDS - 1 :]
    factor = jnp.exp(rate_ref[...] * jnp.tanh(heat))
    scaled = (change * factor).astype(jnp.bfloat16)
    is_heat = lax.broadcasted_iota(jnp.int32, change.shape, 0) == FIELDS - 1
    out = jnp.where(is_heat, change.astype(jnp.bfloat16), scaled)
    for r in range(rows):
        o_ref[r] = out[:, r * CHUNK : (r + 1) * CHUNK]

def surrogate_rows(x, weight_in, bias_in, weight_mid, bias_mid, weight_out, bias_out, rate):
    rows = x.shape[0]
    full = lambda shape: pl.BlockSpec(shape, lambda i: (0,) * len(shape))
    return pl.pallas_call(
        mlp_kernel,
        grid=(rows // ROW_BLOCK,),
        in_specs=[pl.BlockSpec((ROW_BLOCK, FIELDS, CHUNK), lambda i: (i, 0, 0)),
                  full(weight_in.shape), full(bias_in.shape), full(weight_mid.shape), full(bias_mid.shape),
                  full(weight_out.shape), full(bias_out.shape), full(rate.shape)],
        out_specs=pl.BlockSpec((ROW_BLOCK, FIELDS, CHUNK), lambda i: (i, 0, 0)),
        out_shape=jax.ShapeDtypeStruct((rows, FIELDS, CHUNK), jnp.bfloat16),
    )(x, weight_in, bias_in, weight_mid, bias_mid, weight_out, bias_out, rate)


def on_device(
    fields,
    zone_ids,
    diffusivity,
    heat_rate,
    weight_in,
    bias_in,
    weight_mid,
    bias_mid,
    weight_out,
    bias_out,
):
    count_here, rows_here, columns = fields.shape
    coefs = lookup(zone_ids, diffusivity)
    stacked = with_halo(jnp.concatenate([fields, coefs], 0), "space", HALO)
    fields_ext = stacked[:count_here]
    coef_pad = pad_rows(stacked[count_here:])
    first_row = lax.axis_index("space") * rows_here - HALO
    global_row = first_row + lax.broadcasted_iota(jnp.int32, (1, rows_here + 2 * HALO, 1), 1)
    inside = (global_row >= 0) & (global_row < rows_here * lax.axis_size("space"))
    state = fields_ext
    for number in range(SWEEPS):
        state = relax_step(pad_rows(state), fields_ext, coef_pad, RELAX_WEIGHTS[number])
        state = jnp.where(inside, state, jnp.float32(0.0))
    state = state[:, HALO : HALO + rows_here]

    chunks = columns // CHUNK
    outgoing = state[0].reshape(rows_here, chunks, CHUNK).transpose(1, 0, 2).astype(jnp.bfloat16)
    incoming = lax.all_to_all(outgoing, "field", 0, 0, tiled=True)
    rate = jnp.concatenate([heat_rate, jnp.zeros((FIELDS - heat_rate.shape[0],), jnp.float32)])
    delta = surrogate_rows(
        incoming.transpose(1, 0, 2),
        weight_in,
        bias_in[None],
        weight_mid,
        bias_mid[None],
        weight_out,
        bias_out[None],
        rate[:, None],
    )
    returned = lax.all_to_all(delta.transpose(1, 0, 2), "field", 0, 0, tiled=True)
    returned = returned.transpose(1, 0, 2).reshape(1, rows_here, columns)
    return state + returned.astype(jnp.float32)


def solution(mesh):
    return jax.shard_map(
        on_device,
        mesh=mesh,
        in_specs=(
            P("field", "space", None),
            P("space", None),
            P("field", None),
            P(),
            P(),
            P(),
            P(),
            P(),
            P(),
            P(),
        ),
        out_specs=P("field", "space", None),
        check_vma=False,
    )
```
